32 devices in a mesh: groups: 2 (over y), video: 4 (over z), tensor: 4 (over x, core).
Axes of the slice: x: 2, y: 2, z: 4, core: 2. Of those that a mesh axis runs over, the one named last changes fastest.
Arguments:
- frames: bfloat16 [24, 256, 6144], P(('groups', 'video')), parts along dimension 0, may hold values from -610 to 610
- frame_video: int32 [24], P(('groups', 'video')), parts along dimension 0, may hold values from 0 to 3, never falling along the last dimension, each value on 1 to 6 neighbouring positions
- qkv_weight: bfloat16 [6144, 3, 3072], P('video', None, 'tensor'), may hold values from -0.078125 to 0.078125
- conn_weight: bfloat16 [3072, 3, 4096], P('tensor', None, 'video'), may hold values from -6 to 6
Outputs:
- summary: bfloat16 [384, 4096], P(('groups', 'video'), 'tensor'), parts along dimension 0
The draws below stay inside these ranges and needn't reach their ends.
There are 2 independent parts, one for each index of `groups`. The reference program is written for one: setup_inputs(seed, part) draws one part's arguments, and reference() takes and returns one part's arrays. A program takes and returns all parts, laid end to end along the dimension named above; an argument that names none is the same for every part. Nothing has to cross between parts.
All inputs are finite; a program needn't handle non-finite values.
Results may differ from the reference program's by a relative error of at most 0.009.
Values may be sent and summed in bfloat16 or wider, within the bound.
No kernel may reach another device: no remote copies, remote signals or barrier semaphores. Data moves between devices by JAX's collectives and lax.ppermute only.
A program may use at most 192 MiB of HBM per device.

```python
import math
import jax
import jax.numpy as jnp
import numpy as np
from jax import lax

D = 6144
HD = 128
HEADS = 24
T_HEADS = 32
PATCH = 256
POOL = 16
VIDS = 4
TW = 4096
FRAMES = 12
MAXLEN = 6


def draw_frames(key, part):
    keys = jax.random.split(key, 5)
    shape = (FRAMES, PATCH, D)
    base = jnp.clip(jax.random.normal(keys[0], shape, jnp.float32), -6.0, 6.0)
    col_scale = jnp.exp(jax.random.uniform(keys[1], (D,), jnp.float32, 0.0, math.log(10.0)))
    offset = jnp.clip(jax.random.normal(keys[2], (FRAMES, PATCH, 1), jnp.float32), -4.0, 4.0) * 2.0
    row_scale = jnp.exp(jax.random.uniform(keys[4], (FRAMES, PATCH, 1), jnp.float32, 0.0, math.log(10.0)))
    values = base * col_scale * row_scale + offset
    return values.astype(jnp.bfloat16)


def level_of(stream_key, dims, shards, smallest, high):
    factor_of, own = 1.0, jax.random.fold_in(stream_key, 6)
    for position, blocks in shards:
        heights = jnp.exp(jax.random.uniform(jax.random.fold_in(own, position), (blocks,), jnp.float32, smallest / len(shards), high / len(shards)))
        factor_of = factor_of * jnp.repeat(heights, dims[position] // blocks).reshape([-1 if axis == position else 1 for axis in range(len(dims))])
    return factor_of


def split_up(number_of, total, reach, slope):
    weights = [(1 << 20) // math.isqrt(standing ** slope) + 1 for standing in range(2, number_of + 1)]
    spare, counts = total - reach - (number_of - 1), [1] * (number_of - 1)
    while spare > 0:
        movable = [i for i in range(number_of - 1) if counts[i] < reach]
        mass, left = sum([weights[i] for i in movable]), spare
        for i in movable:
            extra = min(reach - counts[i], max(1, left * weights[i] // mass), spare)
            counts[i] = counts[i] + extra
            spare = spare - extra
    return np.array([reach] + counts)


def uneven_parts(rng, amount, total, bound, lean):
    if amount == 2:
        one = jax.random.randint(rng, (), max(1, total - bound), min(bound, total - 1) + 1)
        return jnp.stack([one, total - one])
    tallies = jnp.asarray(split_up(amount, total, bound, lean), jnp.int32)
    couples = (amount - 1) // 2
    donor, sink = tallies[1:1 + 2 * couples:2], tallies[2:2 + 2 * couples:2]
    margin = jnp.minimum(donor - 1, bound - sink)
    moved = jax.random.randint(jax.random.fold_in(rng, 1), (couples,), 0, 1 << 20) % (margin + 1)
    tallies = tallies.at[1:1 + 2 * couples:2].set(donor - moved).at[2:2 + 2 * couples:2].set(sink + moved)
    return tallies[jax.random.permutation(jax.random.fold_in(rng, 2), amount)]


def centred(rng, dims, width, bound, cuts=(), kind=jnp.bfloat16):
    drawn = jax.random.normal(rng, dims, jnp.float32) * width
    if len(cuts) > 0:
        drawn = level_of(rng, dims, cuts, -0.22, 0.18) * drawn
    return jnp.clip(drawn, min=-bound, max=bound).astype(kind)


def setup_inputs(seed: int = 0, part: int = 0) -> dict:
    key_of = jax.random.split(jax.random.key(seed), 5)
    own_keys = jax.random.split(jax.random.fold_in(key_of[4], part), 5)
    frames = draw_frames(jax.random.fold_in(jax.random.fold_in(key_of[4], part), 71), part)
    frame_video = jnp.searchsorted(jnp.cumsum(uneven_parts(own_keys[1], VIDS, FRAMES, MAXLEN, 2)), jnp.arange(FRAMES), side="right").astype(jnp.int32)
    qkv_weight = centred(key_of[2], (D, 3, HEADS * HD), D ** -0.5, 0.078125, ((0, 4), (2, 4)))
    conn_weight = centred(key_of[3], (HEADS * HD, 3, TW), 1.0, 6.0, ((0, 4), (2, 4)))
    return dict(frames=frames, frame_video=frame_video, qkv_weight=qkv_weight, conn_weight=conn_weight)


def rms_norm(values):
    return values * lax.rsqrt(lax.optimization_barrier(jnp.mean(values * values, axis=-1, keepdims=True)) + 1e-06)

def to_half(values):
    return lax.optimization_barrier(values.astype(jnp.bfloat16)).astype(jnp.float32)

def reference(frames, frame_video, qkv_weight, conn_weight):
    scale = 1.0 / math.sqrt(HD)
    blocks = math.isqrt(POOL)
    inner = math.isqrt(PATCH) // blocks
    wide = frames.astype(jnp.float32)
    center = wide - lax.optimization_barrier(jnp.mean(wide, axis=-1, keepdims=True))
    normed = center * lax.rsqrt(lax.optimization_barrier(jnp.mean(center * center, axis=-1, keepdims=True)) + 1e-06)
    normed = normed.astype(jnp.bfloat16).reshape(FRAMES * PATCH, D)
    proj = jnp.dot(normed, qkv_weight.reshape(D, 3 * HEADS * HD), preferred_element_type=jnp.float32)
    proj = proj.reshape(FRAMES, PATCH, 3, HEADS, HD)

    def frame_attend(block):
        query = to_half(rms_norm(block[:, 0]))
        keys = to_half(rms_norm(block[:, 1]))
        values = to_half(block[:, 2])
        scores = jnp.einsum('phd,khd->hpk', query, keys) * scale
        probs = jnp.exp(scores)
        probs = to_half(probs / lax.optimization_barrier(jnp.sum(probs, axis=-1, keepdims=True)))
        attended = jnp.einsum('hpk,khd->phd', probs, values)
        grid = attended.reshape(blocks, inner, blocks, inner, HEADS, HD)
        return lax.optimization_barrier(jnp.mean(grid, axis=(1, 3))).reshape(POOL, HEADS * HD)
    pooled = lax.map(frame_attend, proj).reshape(FRAMES * POOL, HEADS * HD).astype(jnp.bfloat16)
    rows = FRAMES * POOL
    clip_proj = jnp.dot(pooled, conn_weight.reshape(HEADS * HD, 3 * TW), preferred_element_type=jnp.float32)
    clip_proj = clip_proj.reshape(rows, 3, T_HEADS, HD)
    tquery = to_half(rms_norm(clip_proj[:, 0]))
    tkey = to_half(rms_norm(clip_proj[:, 1]))
    tvalue = to_half(clip_proj[:, 2])
    seg_rows = jnp.repeat(frame_video, POOL)
    frame_rows = jnp.arange(rows, dtype=jnp.int32) // POOL
    allowed = (seg_rows[:, None] == seg_rows[None, :]) & (frame_rows[None, :] <= frame_rows[:, None])
    scores = jnp.einsum('rhd,khd->hrk', tquery, tkey) * scale
    weights = jnp.where(allowed[None], jnp.exp(scores), jnp.float32(0.0))
    numer = jnp.einsum('hrk,khd->rhd', to_half(weights), tvalue)
    denom = lax.optimization_barrier(jnp.sum(weights, axis=-1))
    summary = numer / jnp.transpose(denom)[:, :, None]
    return summary.reshape(rows, TW).astype(jnp.bfloat16)
```

```python
import math

import jax
import jax.numpy as jnp
from jax import lax
from jax.sharding import PartitionSpec as P

HD = 128
PATCH = 256
POOL = 16


def rms_norm(values):
    return values * lax.rsqrt(jnp.mean(values * values, axis=-1, keepdims=True) + 1e-06)


def per_device(frames, frame_video, qkv_weight, conn_weight):
    scale = 1.0 / math.sqrt(HD)
    blocks = math.isqrt(POOL)
    inner = math.isqrt(PATCH) // blocks
    nframes = frames.shape[0]
    patch_rows = nframes * PATCH
    n_video = lax.axis_size("video")
    n_groups = lax.axis_size("groups")
    wide = frames.astype(jnp.float32)
    center = wide - jnp.mean(wide, axis=-1, keepdims=True)
    normed = center * lax.rsqrt(jnp.mean(center * center, axis=-1, keepdims=True) + 1e-06)
    normed = normed.astype(jnp.bfloat16).reshape(patch_rows, frames.shape[2])
    local_cols = qkv_weight.shape[1] * qkv_weight.shape[2]
    share = qkv_weight.shape[0] // n_groups
    mine = lax.dynamic_slice_in_dim(qkv_weight, lax.axis_index("groups") * share, share, axis=0)
    piece = lax.all_gather(mine, ("video", "groups"), axis=0, tiled=True)
    proj = jnp.dot(
        normed, piece.reshape(piece.shape[0], local_cols), preferred_element_type=jnp.float32
    )
    heads_local = qkv_weight.shape[2] // HD
    proj = proj.reshape(nframes, PATCH, 3, heads_local, HD)
    query = rms_norm(proj[:, :, 0]).astype(jnp.bfloat16)
    keys = rms_norm(proj[:, :, 1]).astype(jnp.bfloat16)
    values = proj[:, :, 2].astype(jnp.bfloat16)
    scores = jnp.einsum("fphd,fkhd->fhpk", query, keys, preferred_element_type=jnp.float32) * scale
    probs = jnp.exp(scores)
    probs = (probs / jnp.sum(probs, axis=-1, keepdims=True)).astype(jnp.bfloat16)
    attended = jnp.einsum("fhpk,fkhd->fphd", probs, values, preferred_element_type=jnp.float32)
    grid = attended.reshape(nframes, blocks, inner, blocks, inner, heads_local, HD)
    pooled = (
        jnp.mean(grid, axis=(2, 4)).reshape(nframes * POOL, heads_local * HD).astype(jnp.bfloat16)
    )
    pooled_all = lax.all_gather(pooled, "video", axis=0, tiled=True)
    rows = pooled_all.shape[0]
    partial_proj = jnp.einsum(
        "rc,ckt->rkt", pooled_all, conn_weight, preferred_element_type=jnp.float32
    )
    clip_rows = lax.psum_scatter(
        partial_proj.astype(jnp.bfloat16), "tensor", scatter_dimension=0, tiled=True
    )
    clip_rows = lax.all_gather(clip_rows, "video", axis=2, tiled=True)
    clip_proj = lax.all_to_all(clip_rows, "tensor", 2, 0, tiled=True).astype(jnp.float32)
    t_heads = clip_proj.shape[2] // HD
    out_rows = rows // n_video
    first = lax.axis_index("video") * out_rows
    own = lax.dynamic_slice_in_dim(clip_proj[:, 0], first, out_rows, axis=0)
    tquery = rms_norm(own.reshape(out_rows, t_heads, HD)).astype(jnp.bfloat16)
    tkey = rms_norm(clip_proj[:, 1].reshape(rows, t_heads, HD)).astype(jnp.bfloat16)
    tvalue = clip_proj[:, 2].reshape(rows, t_heads, HD).astype(jnp.bfloat16)
    video_all = lax.all_gather(frame_video, "video", axis=0, tiled=True)
    seg_rows = jnp.repeat(video_all, POOL)
    row_frame = jnp.arange(rows, dtype=jnp.int32) // POOL
    own_seg = lax.dynamic_slice_in_dim(seg_rows, first, out_rows)
    own_frame = lax.dynamic_slice_in_dim(row_frame, first, out_rows)
    allowed = (seg_rows[None, :] == own_seg[:, None]) & (row_frame[None, :] <= own_frame[:, None])
    logits = jnp.einsum("rhd,khd->hrk", tquery, tkey, preferred_element_type=jnp.float32) * scale
    weights = jnp.where(allowed[None], jnp.exp(logits), jnp.float32(0.0))
    numer = jnp.einsum(
        "hrk,khd->rhd", weights.astype(jnp.bfloat16), tvalue, preferred_element_type=jnp.float32
    )
    denom = jnp.sum(weights, axis=-1)
    summary = numer / jnp.transpose(denom)[:, :, None]
    return summary.reshape(out_rows, t_heads * HD).astype(jnp.bfloat16)


def solution(mesh):
    return jax.shard_map(
        per_device,
        mesh=mesh,
        in_specs=(
            P(("groups", "video"), None, None),
            P(("groups", "video")),
            P("video", None, "tensor"),
            P("tensor", None, "video"),
        ),
        out_specs=P(("groups", "video"), "tensor"),
        check_vma=False,
    )
```

```python
import math

import jax
import jax.numpy as jnp
from jax import lax
from jax.sharding import PartitionSpec as P

HD = 128
PATCH = 256
POOL = 16


def rms_norm(values):
    return values * lax.rsqrt(jnp.mean(values * values, axis=-1, keepdims=True) + 1e-06)


SPLIT = 1


def project(normed, qkv_weight, n_video, n_groups):
    assert n_groups == 2
    v = lax.axis_index("video")
    g = lax.axis_index("groups")
    local_rows, parts, cols = qkv_weight.shape
    half = local_rows // 2
    srows = half // SPLIT
    n = normed.shape[0]
    blocks = normed.reshape(n, n_video, 2, SPLIT, srows)
    outs = []
    for j in range(parts):
        acc = None
        for s in range(SPLIT):
            mine = lax.dynamic_slice_in_dim(qkv_weight[:, j], g * half + s * srows, srows, axis=0)
            other = lax.dynamic_slice_in_dim(qkv_weight[:, j], (1 - g) * half + s * srows, srows, axis=0)
            gathered = lax.all_gather(mine, "video", axis=0, tiled=False)
            twice = jnp.concatenate([gathered, gathered], axis=0)
            onward = lax.dynamic_slice_in_dim(twice, v + 1, n_video - 1, axis=0)
            received = lax.ppermute(onward, "groups", [(0, 1), (1, 0)])
            cut = blocks[:, :, :, s]
            own_half = lax.dynamic_index_in_dim(cut, g, axis=2, keepdims=False)
            other_half = lax.dynamic_index_in_dim(cut, 1 - g, axis=2, keepdims=False)
            own_piece = lax.dynamic_index_in_dim(other_half, v, axis=1, keepdims=False)
            rolled = lax.dynamic_slice_in_dim(
                jnp.concatenate([other_half, other_half], axis=1), v + 1, n_video - 1, axis=1
            )
            part = jnp.dot(own_piece, other, preferred_element_type=jnp.float32)
            part = part + jnp.einsum(
                "nvd,vdc->nc", own_half, gathered, preferred_element_type=jnp.float32
            )
            part = part + jnp.einsum(
                "nvd,vdc->nc", rolled, received, preferred_element_type=jnp.float32
            )
            acc = part if acc is None else acc + part
        outs.append(acc)
    return jnp.stack(outs, axis=1)


def per_device(frames, frame_video, qkv_weight, conn_weight):
    scale = 1.0 / math.sqrt(HD)
    blocks = math.isqrt(POOL)
    inner = math.isqrt(PATCH) // blocks
    nframes = frames.shape[0]
    patch_rows = nframes * PATCH
    n_video = lax.axis_size("video")
    n_groups = lax.axis_size("groups")
    wide = frames.astype(jnp.float32)
    center = wide - jnp.mean(wide, axis=-1, keepdims=True)
    normed = center * lax.rsqrt(jnp.mean(center * center, axis=-1, keepdims=True) + 1e-06)
    normed = normed.astype(jnp.bfloat16).reshape(patch_rows, frames.shape[2])
    heads_local = qkv_weight.shape[2] // HD
    proj = project(normed, qkv_weight, n_video, n_groups).reshape(nframes, PATCH, 3, heads_local, HD)
    query = rms_norm(proj[:, :, 0]).astype(jnp.bfloat16)
    keys = rms_norm(proj[:, :, 1]).astype(jnp.bfloat16)
    values = proj[:, :, 2].astype(jnp.bfloat16)
    scores = jnp.einsum("fphd,fkhd->fhpk", query, keys, preferred_element_type=jnp.float32) * scale
    probs = jnp.exp(scores)
    probs = (probs / jnp.sum(probs, axis=-1, keepdims=True)).astype(jnp.bfloat16)
    attended = jnp.einsum("fhpk,fkhd->fphd", probs, values, preferred_element_type=jnp.float32)
    grid = attended.reshape(nframes, blocks, inner, blocks, inner, heads_local, HD)
    pooled = (
        jnp.mean(grid, axis=(2, 4)).reshape(nframes * POOL, heads_local * HD).astype(jnp.bfloat16)
    )
    pooled_all = lax.all_gather(pooled, "video", axis=0, tiled=True)
    rows = pooled_all.shape[0]
    partial_proj = jnp.einsum(
        "rc,ckt->rkt", pooled_all, conn_weight, preferred_element_type=jnp.float32
    )
    clip_rows = lax.psum_scatter(
        partial_proj.astype(jnp.bfloat16), "tensor", scatter_dimension=0, tiled=True
    )
    clip_rows = lax.all_gather(clip_rows, "video", axis=2, tiled=True)
    clip_proj = lax.all_to_all(clip_rows, "tensor", 2, 0, tiled=True).astype(jnp.float32)
    t_heads = clip_proj.shape[2] // HD
    out_rows = rows // n_video
    first = lax.axis_index("video") * out_rows
    own = lax.dynamic_slice_in_dim(clip_proj[:, 0], first, out_rows, axis=0)
    tquery = rms_norm(own.reshape(out_rows, t_heads, HD)).astype(jnp.bfloat16)
    tkey = rms_norm(clip_proj[:, 1].reshape(rows, t_heads, HD)).astype(jnp.bfloat16)
    tvalue = clip_proj[:, 2].reshape(rows, t_heads, HD).astype(jnp.bfloat16)
    video_all = lax.all_gather(frame_video, "video", axis=0, tiled=True)
    seg_rows = jnp.repeat(video_all, POOL)
    row_frame = jnp.arange(rows, dtype=jnp.int32) // POOL
    own_seg = lax.dynamic_slice_in_dim(seg_rows, first, out_rows)
    own_frame = lax.dynamic_slice_in_dim(row_frame, first, out_rows)
    allowed = (seg_rows[None, :] == own_seg[:, None]) & (row_frame[None, :] <= own_frame[:, None])
    logits = jnp.einsum("rhd,khd->hrk", tquery, tkey, preferred_element_type=jnp.float32) * scale
    weights = jnp.where(allowed[None], jnp.exp(logits), jnp.float32(0.0))
    numer = jnp.einsum(
        "hrk,khd->rhd", weights.astype(jnp.bfloat16), tvalue, preferred_element_type=jnp.float32
    )
    denom = jnp.sum(weights, axis=-1)
    summary = numer / jnp.transpose(denom)[:, :, None]
    return summary.reshape(out_rows, t_heads * HD).astype(jnp.bfloat16)


def solution(mesh):
    return jax.shard_map(
        per_device,
        mesh=mesh,
        in_specs=(
            P(("groups", "video"), None, None),
            P(("groups", "video")),
            P("video", None, "tensor"),
            P("tensor", None, "video"),
        ),
        out_specs=P(("groups", "video"), "tensor"),
        check_vma=False,
    )
```

```python
import math

import jax
import jax.numpy as jnp
from jax import lax
from jax.sharding import PartitionSpec as P

HD = 128
PATCH = 256
POOL = 16


def rms_norm(values):
    return values * lax.rsqrt(jnp.mean(values * values, axis=-1, keepdims=True) + 1e-06)


SPLIT = 2


def project(normed, qkv_weight, n_video, n_groups):
    assert n_groups == 2
    v = lax.axis_index("video")
    g = lax.axis_index("groups")
    local_rows, parts, cols = qkv_weight.shape
    half = local_rows // 2
    srows = half // SPLIT
    n = normed.shape[0]
    blocks = normed.reshape(n, n_video, 2, SPLIT, srows)
    outs = []
    for j in range(parts):
        acc = None
        for s in range(SPLIT):
            mine = lax.dynamic_slice_in_dim(qkv_weight[:, j], g * half + s * srows, srows, axis=0)
            other = lax.dynamic_slice_in_dim(qkv_weight[:, j], (1 - g) * half + s * srows, srows, axis=0)
            gathered = lax.all_gather(mine, "video", axis=0, tiled=False)
            twice = jnp.concatenate([gathered, gathered], axis=0)
            onward = lax.dynamic_slice_in_dim(twice, v + 1, n_video - 1, axis=0)
            received = lax.ppermute(onward, "groups", [(0, 1), (1, 0)])
            cut = blocks[:, :, :, s]
            own_half = lax.dynamic_index_in_dim(cut, g, axis=2, keepdims=False)
            other_half = lax.dynamic_index_in_dim(cut, 1 - g, axis=2, keepdims=False)
            own_piece = lax.dynamic_index_in_dim(other_half, v, axis=1, keepdims=False)
            rolled = lax.dynamic_slice_in_dim(
                jnp.concatenate([other_half, other_half], axis=1), v + 1, n_video - 1, axis=1
            )
            part = jnp.dot(own_piece, other, preferred_element_type=jnp.float32)
            part = part + jnp.einsum(
                "nvd,vdc->nc", own_half, gathered, preferred_element_type=jnp.float32
            )
            part = part + jnp.einsum(
                "nvd,vdc->nc", rolled, received, preferred_element_type=jnp.float32
            )
            acc = part if acc is None else acc + part
        outs.append(acc)
    return jnp.stack(outs, axis=1)


def per_device(frames, frame_video, qkv_weight, conn_weight):
    scale = 1.0 / math.sqrt(HD)
    blocks = math.isqrt(POOL)
    inner = math.isqrt(PATCH) // blocks
    nframes = frames.shape[0]
    patch_rows = nframes * PATCH
    n_video = lax.axis_size("video")
    n_groups = lax.axis_size("groups")
    wide = frames.astype(jnp.float32)
    center = wide - jnp.mean(wide, axis=-1, keepdims=True)
    normed = center * lax.rsqrt(jnp.mean(center * center, axis=-1, keepdims=True) + 1e-06)
    normed = normed.astype(jnp.bfloat16).reshape(patch_rows, frames.shape[2])
    video_all = lax.all_gather(frame_video, "video", axis=0, tiled=True)
    video_all, normed = lax.optimization_barrier((video_all, normed))
    heads_local = qkv_weight.shape[2] // HD
    proj = project(normed, qkv_weight, n_video, n_groups).reshape(nframes, PATCH, 3, heads_local, HD)
    query = rms_norm(proj[:, :, 0]).astype(jnp.bfloat16)
    keys = rms_norm(proj[:, :, 1]).astype(jnp.bfloat16)
    values = proj[:, :, 2].astype(jnp.bfloat16)
    scores = jnp.einsum("fphd,fkhd->fhpk", query, keys, preferred_element_type=jnp.float32) * scale
    probs = jnp.exp(scores)
    probs = (probs / jnp.sum(probs, axis=-1, keepdims=True)).astype(jnp.bfloat16)
    attended = jnp.einsum("fhpk,fkhd->fphd", probs, values, preferred_element_type=jnp.float32)
    grid = attended.reshape(nframes, blocks, inner, blocks, inner, heads_local, HD)
    pooled = (
        jnp.mean(grid, axis=(2, 4)).reshape(nframes * POOL, heads_local * HD).astype(jnp.bfloat16)
    )
    pooled_all = lax.all_gather(pooled, "video", axis=0, tiled=True)
    rows = pooled_all.shape[0]
    partial_proj = jnp.einsum(
        "rc,ckt->rkt", pooled_all, conn_weight, preferred_element_type=jnp.float32
    )
    n_tensor = lax.axis_size("tensor")
    if n_video == n_tensor:
        summed = lax.psum(partial_proj.astype(jnp.bfloat16), "tensor")
        swap = [(a * n_tensor + b, b * n_tensor + a) for a in range(n_video) for b in range(n_tensor)]
        clip_proj = lax.ppermute(summed, ("video", "tensor"), swap).astype(jnp.float32)
    else:
        clip_rows = lax.psum_scatter(
            partial_proj.astype(jnp.bfloat16), "tensor", scatter_dimension=0, tiled=True
        )
        clip_rows = lax.all_gather(clip_rows, "video", axis=2, tiled=True)
        clip_proj = lax.all_to_all(clip_rows, "tensor", 2, 0, tiled=True).astype(jnp.float32)
    t_heads = clip_proj.shape[2] // HD
    out_rows = rows // n_video
    first = lax.axis_index("video") * out_rows
    own = lax.dynamic_slice_in_dim(clip_proj[:, 0], first, out_rows, axis=0)
    tquery = rms_norm(own.reshape(out_rows, t_heads, HD)).astype(jnp.bfloat16)
    tkey = rms_norm(clip_proj[:, 1].reshape(rows, t_heads, HD)).astype(jnp.bfloat16)
    tvalue = clip_proj[:, 2].reshape(rows, t_heads, HD).astype(jnp.bfloat16)
    seg_rows = jnp.repeat(video_all, POOL)
    row_frame = jnp.arange(rows, dtype=jnp.int32) // POOL
    own_seg = lax.dynamic_slice_in_dim(seg_rows, first, out_rows)
    own_frame = lax.dynamic_slice_in_dim(row_frame, first, out_rows)
    allowed = (seg_rows[None, :] == own_seg[:, None]) & (row_frame[None, :] <= own_frame[:, None])
    logits = jnp.einsum("rhd,khd->hrk", tquery, tkey, preferred_element_type=jnp.float32) * scale
    weights = jnp.where(allowed[None], jnp.exp(logits), jnp.float32(0.0))
    numer = jnp.einsum(
        "hrk,khd->rhd", weights.astype(jnp.bfloat16), tvalue, preferred_element_type=jnp.float32
    )
    denom = jnp.sum(weights, axis=-1)
    summary = numer / jnp.transpose(denom)[:, :, None]
    return summary.reshape(out_rows, t_heads * HD).astype(jnp.bfloat16)


def solution(mesh):
    return jax.shard_map(
        per_device,
        mesh=mesh,
        in_specs=(
            P(("groups", "video"), None, None),
            P(("groups", "video")),
            P("video", None, "tensor"),
            P("tensor", None, "video"),
        ),
        out_specs=P(("groups", "video"), "tensor"),
        check_vma=False,
    )
```

```python
import math

import jax
import jax.numpy as jnp
from jax import lax
from jax.sharding import PartitionSpec as P

HD = 128
PATCH = 256
POOL = 16


def rms_norm(values):
    return values * lax.rsqrt(jnp.mean(values * values, axis=-1, keepdims=True) + 1e-06)


def head_chunks(heads):
    if heads >= 4 and heads % 2 == 0:
        return [1] + [2] * ((heads - 2) // 2) + [1]
    return [1] * heads


def moved_weights(chunk, n_video):
    v = lax.axis_index("video")
    g = lax.axis_index("groups")
    half = chunk.shape[0] // 2
    mine = lax.dynamic_slice_in_dim(chunk, g * half, half, axis=0)
    other = lax.dynamic_slice_in_dim(chunk, (1 - g) * half, half, axis=0)
    gathered = lax.all_gather(mine, "video", axis=0, tiled=False)
    twice = jnp.concatenate([gathered, gathered], axis=0)
    onward = lax.dynamic_slice_in_dim(twice, v + 1, n_video - 1, axis=0)
    received = lax.ppermute(onward, "groups", [(0, 1), (1, 0)])
    return other, gathered, received


def attend(proj, nframes, heads, scale, blocks, inner):
    proj = proj.reshape(nframes, PATCH, 3, heads, HD)
    query = rms_norm(proj[:, :, 0]).astype(jnp.bfloat16)
    keys = rms_norm(proj[:, :, 1]).astype(jnp.bfloat16)
    values = proj[:, :, 2].astype(jnp.bfloat16)
    scores = jnp.einsum("fphd,fkhd->fhpk", query, keys, preferred_element_type=jnp.float32) * scale
    probs = jnp.exp(scores)
    probs = (probs / jnp.sum(probs, axis=-1, keepdims=True)).astype(jnp.bfloat16)
    attended = jnp.einsum("fhpk,fkhd->fphd", probs, values, preferred_element_type=jnp.float32)
    grid = attended.reshape(nframes, blocks, inner, blocks, inner, heads, HD)
    return jnp.mean(grid, axis=(2, 4)).reshape(nframes * POOL, heads * HD).astype(jnp.bfloat16)


def per_device(frames, frame_video, qkv_weight, conn_weight):
    scale = 1.0 / math.sqrt(HD)
    blocks = math.isqrt(POOL)
    inner = math.isqrt(PATCH) // blocks
    nframes = frames.shape[0]
    patch_rows = nframes * PATCH
    n_video = lax.axis_size("video")
    assert lax.axis_size("groups") == 2
    v = lax.axis_index("video")
    g = lax.axis_index("groups")
    wide = frames.astype(jnp.float32)
    center = wide - jnp.mean(wide, axis=-1, keepdims=True)
    normed = center * lax.rsqrt(jnp.mean(center * center, axis=-1, keepdims=True) + 1e-06)
    normed = normed.astype(jnp.bfloat16).reshape(patch_rows, frames.shape[2])
    half = qkv_weight.shape[0] // 2
    cut = normed.reshape(patch_rows, n_video, 2, half)
    own_half = lax.dynamic_index_in_dim(cut, g, axis=2, keepdims=False)
    other_half = lax.dynamic_index_in_dim(cut, 1 - g, axis=2, keepdims=False)
    own_piece = lax.dynamic_index_in_dim(other_half, v, axis=1, keepdims=False)
    rolled = lax.dynamic_slice_in_dim(
        jnp.concatenate([other_half, other_half], axis=1), v + 1, n_video - 1, axis=1
    )
    heads_local = qkv_weight.shape[2] // HD
    pooled_parts = []
    first = 0
    for size in head_chunks(heads_local):
        chunk = qkv_weight[:, :, first * HD:(first + size) * HD]
        first += size
        width = 3 * size * HD
        other, gathered, received = moved_weights(chunk, n_video)
        proj = jnp.dot(own_piece, other.reshape(half, width), preferred_element_type=jnp.float32)
        proj = proj + jnp.einsum(
            "nvd,vdc->nc", own_half, gathered.reshape(n_video, half, width),
            preferred_element_type=jnp.float32,
        )
        proj = proj + jnp.einsum(
            "nvd,vdc->nc", rolled, received.reshape(n_video - 1, half, width),
            preferred_element_type=jnp.float32,
        )
        pooled_parts.append(attend(proj, nframes, size, scale, blocks, inner))
    pooled = jnp.concatenate(pooled_parts, axis=1)
    pooled_all = lax.all_gather(pooled, "video", axis=0, tiled=True)
    rows = pooled_all.shape[0]
    partial_proj = jnp.einsum(
        "rc,ckt->rkt", pooled_all, conn_weight, preferred_element_type=jnp.float32
    )
    clip_rows = lax.psum_scatter(
        partial_proj.astype(jnp.bfloat16), "tensor", scatter_dimension=0, tiled=True
    )
    clip_rows = lax.all_gather(clip_rows, "video", axis=2, tiled=True)
    clip_proj = lax.all_to_all(clip_rows, "tensor", 2, 0, tiled=True).astype(jnp.float32)
    t_heads = clip_proj.shape[2] // HD
    out_rows = rows // n_video
    start = v * out_rows
    own = lax.dynamic_slice_in_dim(clip_proj[:, 0], start, out_rows, axis=0)
    tquery = rms_norm(own.reshape(out_rows, t_heads, HD)).astype(jnp.bfloat16)
    tkey = rms_norm(clip_proj[:, 1].reshape(rows, t_heads, HD)).astype(jnp.bfloat16)
    tvalue = clip_proj[:, 2].reshape(rows, t_heads, HD).astype(jnp.bfloat16)
    video_all = lax.all_gather(frame_video, "video", axis=0, tiled=True)
    seg_rows = jnp.repeat(video_all, POOL)
    row_frame = jnp.arange(rows, dtype=jnp.int32) // POOL
    own_seg = lax.dynamic_slice_in_dim(seg_rows, start, out_rows)
    own_frame = lax.dynamic_slice_in_dim(row_frame, start, out_rows)
    allowed = (seg_rows[None, :] == own_seg[:, None]) & (row_frame[None, :] <= own_frame[:, None])
    logits = jnp.einsum("rhd,khd->hrk", tquery, tkey, preferred_element_type=jnp.float32) * scale
    weights = jnp.where(allowed[None], jnp.exp(logits), jnp.float32(0.0))
    numer = jnp.einsum(
        "hrk,khd->rhd", weights.astype(jnp.bfloat16), tvalue, preferred_element_type=jnp.float32
    )
    denom = jnp.sum(weights, axis=-1)
    summary = numer / jnp.transpose(denom)[:, :, None]
    return summary.reshape(out_rows, t_heads * HD).astype(jnp.bfloat16)


def solution(mesh):
    return jax.shard_map(
        per_device,
        mesh=mesh,
        in_specs=(
            P(("groups", "video"), None, None),
            P(("groups", "video")),
            P("video", None, "tensor"),
            P("tensor", None, "video"),
        ),
        out_specs=P(("groups", "video"), "tensor"),
        check_vma=False,
    )
```

```python
import math

import jax
import jax.numpy as jnp
from jax import lax
from jax.sharding import PartitionSpec as P

HD = 128
PATCH = 256
POOL = 16


def rms_norm(values):
    return values * lax.rsqrt(jnp.mean(values * values, axis=-1, keepdims=True) + 1e-06)


def head_chunks(heads):
    if heads >= 4 and heads % 2 == 0:
        return [1] + [2] * ((heads - 2) // 2) + [1]
    return [1] * heads


def moved_weights(chunk, n_video):
    v = lax.axis_index("video")
    g = lax.axis_index("groups")
    half = chunk.shape[0] // 2
    mine = lax.dynamic_slice_in_dim(chunk, g * half, half, axis=0)
    other = lax.dynamic_slice_in_dim(chunk, (1 - g) * half, half, axis=0)
    gathered = lax.all_gather(mine, "video", axis=0, tiled=False)
    twice = jnp.concatenate([gathered, gathered], axis=0)
    onward = lax.dynamic_slice_in_dim(twice, v + 1, n_video - 1, axis=0)
    return other, gathered, onward


def forward(onward):
    return lax.ppermute(onward, "groups", [(0, 1), (1, 0)])


def attend(proj, nframes, heads, scale, blocks, inner):
    proj = proj.reshape(nframes, PATCH, 3, heads, HD)
    query = rms_norm(proj[:, :, 0]).astype(jnp.bfloat16)
    keys = rms_norm(proj[:, :, 1]).astype(jnp.bfloat16)
    values = proj[:, :, 2].astype(jnp.bfloat16)
    scores = jnp.einsum("fphd,fkhd->fhpk", query, keys, preferred_element_type=jnp.float32) * scale
    probs = jnp.exp(scores)
    probs = (probs / jnp.sum(probs, axis=-1, keepdims=True)).astype(jnp.bfloat16)
    attended = jnp.einsum("fhpk,fkhd->fphd", probs, values, preferred_element_type=jnp.float32)
    grid = attended.reshape(nframes, blocks, inner, blocks, inner, heads, HD)
    return jnp.mean(grid, axis=(2, 4)).reshape(nframes * POOL, heads * HD).astype(jnp.bfloat16)


def per_device(frames, frame_video, qkv_weight, conn_weight):
    scale = 1.0 / math.sqrt(HD)
    blocks = math.isqrt(POOL)
    inner = math.isqrt(PATCH) // blocks
    nframes = frames.shape[0]
    patch_rows = nframes * PATCH
    n_video = lax.axis_size("video")
    assert lax.axis_size("groups") == 2
    v = lax.axis_index("video")
    g = lax.axis_index("groups")
    heads_local = qkv_weight.shape[2] // HD
    sizes = head_chunks(heads_local)
    first_moved = moved_weights(qkv_weight[:, :, :sizes[0] * HD], n_video)
    onward0, frames = lax.optimization_barrier((first_moved[2], frames))
    wide = frames.astype(jnp.float32)
    center = wide - jnp.mean(wide, axis=-1, keepdims=True)
    normed = center * lax.rsqrt(jnp.mean(center * center, axis=-1, keepdims=True) + 1e-06)
    normed = normed.astype(jnp.bfloat16).reshape(patch_rows, frames.shape[2])
    half = qkv_weight.shape[0] // 2
    cut = normed.reshape(patch_rows, n_video, 2, half)
    own_half = lax.dynamic_index_in_dim(cut, g, axis=2, keepdims=False)
    other_half = lax.dynamic_index_in_dim(cut, 1 - g, axis=2, keepdims=False)
    own_piece = lax.dynamic_index_in_dim(other_half, v, axis=1, keepdims=False)
    rolled = lax.dynamic_slice_in_dim(
        jnp.concatenate([other_half, other_half], axis=1), v + 1, n_video - 1, axis=1
    )
    video_all = lax.all_gather(frame_video, "video", axis=0, tiled=True)
    pooled_parts = []
    first = 0
    for index, size in enumerate(sizes):
        chunk = qkv_weight[:, :, first * HD:(first + size) * HD]
        first += size
        width = 3 * size * HD
        if index == 0:
            other, gathered = first_moved[0], first_moved[1]
            received = forward(onward0)
            video_all, received = lax.optimization_barrier((video_all, received))
        else:
            other, gathered, onward = moved_weights(chunk, n_video)
            received = forward(onward)
        proj = jnp.dot(own_piece, other.reshape(half, width), preferred_element_type=jnp.float32)
        proj = proj + jnp.einsum(
            "nvd,vdc->nc", own_half, gathered.reshape(n_video, half, width),
            preferred_element_type=jnp.float32,
        )
        proj = proj + jnp.einsum(
            "nvd,vdc->nc", rolled, received.reshape(n_video - 1, half, width),
            preferred_element_type=jnp.float32,
        )
        pooled_parts.append(attend(proj, nframes, size, scale, blocks, inner))
    pooled = jnp.concatenate(pooled_parts, axis=1)
    pooled_all = lax.all_gather(pooled, "video", axis=0, tiled=True)
    rows = pooled_all.shape[0]
    partial_proj = jnp.einsum(
        "rc,ckt->rkt", pooled_all, conn_weight, preferred_element_type=jnp.float32
    )
    clip_rows = lax.psum_scatter(
        partial_proj.astype(jnp.bfloat16), "tensor", scatter_dimension=0, tiled=True
    )
    n_tensor = lax.axis_size("tensor")
    clip_rows = lax.all_gather(clip_rows, "video", axis=0, tiled=False)
    sub = n_video // n_tensor
    clip_rows = clip_rows.reshape((n_tensor, sub) + clip_rows.shape[1:])
    clip_proj = lax.all_to_all(clip_rows, "tensor", 0, 0, tiled=False)
    clip_proj = jnp.transpose(clip_proj, (0, 2, 3, 1, 4))
    clip_proj = clip_proj.reshape(rows, 3, -1).astype(jnp.float32)
    t_heads = clip_proj.shape[2] // HD
    out_rows = rows // n_video
    start = v * out_rows
    own = lax.dynamic_slice_in_dim(clip_proj[:, 0], start, out_rows, axis=0)
    tquery = rms_norm(own.reshape(out_rows, t_heads, HD)).astype(jnp.bfloat16)
    tkey = rms_norm(clip_proj[:, 1].reshape(rows, t_heads, HD)).astype(jnp.bfloat16)
    tvalue = clip_proj[:, 2].reshape(rows, t_heads, HD).astype(jnp.bfloat16)
    seg_rows = jnp.repeat(video_all, POOL)
    row_frame = jnp.arange(rows, dtype=jnp.int32) // POOL
    own_seg = lax.dynamic_slice_in_dim(seg_rows, start, out_rows)
    own_frame = lax.dynamic_slice_in_dim(row_frame, start, out_rows)
    allowed = (seg_rows[None, :] == own_seg[:, None]) & (row_frame[None, :] <= own_frame[:, None])
    logits = jnp.einsum("rhd,khd->hrk", tquery, tkey, preferred_element_type=jnp.float32) * scale
    weights = jnp.where(allowed[None], jnp.exp(logits), jnp.float32(0.0))
    numer = jnp.einsum(
        "hrk,khd->rhd", weights.astype(jnp.bfloat16), tvalue, preferred_element_type=jnp.float32
    )
    denom = jnp.sum(weights, axis=-1)
    summary = numer / jnp.transpose(denom)[:, :, None]
    return summary.reshape(out_rows, t_heads * HD).astype(jnp.bfloat16)


def solution(mesh):
    return jax.shard_map(
        per_device,
        mesh=mesh,
        in_specs=(
            P(("groups", "video"), None, None),
            P(("groups", "video")),
            P("video", None, "tensor"),
            P("tensor", None, "video"),
        ),
        out_specs=P(("groups", "video"), "tensor"),
        check_vma=False,
    )
```

```python
import math

import jax
import jax.numpy as jnp
from jax import lax
from jax.sharding import PartitionSpec as P

HD = 128
PATCH = 256
POOL = 16


def rms_norm(values):
    return values * lax.rsqrt(jnp.mean(values * values, axis=-1, keepdims=True) + 1e-06)


def head_chunks(heads):
    if heads >= 4 and heads % 2 == 0:
        return [1] + [2] * ((heads - 2) // 2) + [1]
    return [1] * heads


def moved_weights(chunk, n_video, after=None):
    v = lax.axis_index("video")
    g = lax.axis_index("groups")
    half = chunk.shape[0] // 2
    mine = lax.dynamic_slice_in_dim(chunk, g * half, half, axis=0)
    if after is not None:
        mine, after = lax.optimization_barrier((mine, after))
    other = lax.dynamic_slice_in_dim(chunk, (1 - g) * half, half, axis=0)
    gathered = lax.all_gather(mine, "video", axis=0, tiled=False)
    twice = jnp.concatenate([gathered, gathered], axis=0)
    onward = lax.dynamic_slice_in_dim(twice, v + 1, n_video - 1, axis=0)
    return [other, gathered, onward], after


def forward(onward):
    return lax.ppermute(onward, "groups", [(0, 1), (1, 0)])


def attend(proj, nframes, heads, scale, blocks, inner):
    proj = proj.reshape(nframes, PATCH, 3, heads, HD)
    query = rms_norm(proj[:, :, 0]).astype(jnp.bfloat16)
    keys = rms_norm(proj[:, :, 1]).astype(jnp.bfloat16)
    values = proj[:, :, 2].astype(jnp.bfloat16)
    scores = jnp.einsum("fphd,fkhd->fhpk", query, keys, preferred_element_type=jnp.float32) * scale
    probs = jnp.exp(scores)
    probs = (probs / jnp.sum(probs, axis=-1, keepdims=True)).astype(jnp.bfloat16)
    attended = jnp.einsum("fhpk,fkhd->fphd", probs, values, preferred_element_type=jnp.float32)
    grid = attended.reshape(nframes, blocks, inner, blocks, inner, heads, HD)
    return jnp.mean(grid, axis=(2, 4)).reshape(nframes * POOL, heads * HD).astype(jnp.bfloat16)


def per_device(frames, frame_video, qkv_weight, conn_weight):
    scale = 1.0 / math.sqrt(HD)
    blocks = math.isqrt(POOL)
    inner = math.isqrt(PATCH) // blocks
    nframes = frames.shape[0]
    patch_rows = nframes * PATCH
    n_video = lax.axis_size("video")
    assert lax.axis_size("groups") == 2
    v = lax.axis_index("video")
    g = lax.axis_index("groups")
    heads_local = qkv_weight.shape[2] // HD
    sizes = head_chunks(heads_local)
    moved = []
    first = 0
    for size in sizes:
        chunk = qkv_weight[:, :, first * HD:(first + size) * HD]
        first += size
        if len(moved) == len(sizes) - 1 and len(sizes) > 2:
            whole_rows, moved[-1][1] = lax.optimization_barrier((chunk, moved[-1][1]))
            step = [lax.all_gather(whole_rows, "video", axis=0, tiled=True), None, None]
        elif moved:
            step, moved[-1][1] = moved_weights(chunk, n_video, after=moved[-1][1])
        else:
            step, _ = moved_weights(chunk, n_video)
            step.append(forward(step[2]))
            step[3], frames = lax.optimization_barrier((step[3], frames))
        moved.append(step)
    wide = frames.astype(jnp.float32)
    center = wide - jnp.mean(wide, axis=-1, keepdims=True)
    normed = center * lax.rsqrt(jnp.mean(center * center, axis=-1, keepdims=True) + 1e-06)
    normed = normed.astype(jnp.bfloat16).reshape(patch_rows, frames.shape[2])
    half = qkv_weight.shape[0] // 2
    cut = normed.reshape(patch_rows, n_video, 2, half)
    own_half = lax.dynamic_index_in_dim(cut, g, axis=2, keepdims=False)
    other_half = lax.dynamic_index_in_dim(cut, 1 - g, axis=2, keepdims=False)
    own_piece = lax.dynamic_index_in_dim(other_half, v, axis=1, keepdims=False)
    rolled = lax.dynamic_slice_in_dim(
        jnp.concatenate([other_half, other_half], axis=1), v + 1, n_video - 1, axis=1
    )
    video_all = lax.all_gather(frame_video, "video", axis=0, tiled=True)
    pooled_parts = []
    for index, size in enumerate(sizes):
        width = 3 * size * HD
        if moved[index][1] is None:
            full = moved[index][0].reshape(n_video * 2 * half, width)
            proj = jnp.dot(normed, full, preferred_element_type=jnp.float32)
            pooled_parts.append(attend(proj, nframes, size, scale, blocks, inner))
            continue
        other, gathered, onward = moved[index][:3]
        if index == 0:
            received = moved[index][3]
            video_all, received = lax.optimization_barrier((video_all, received))
        else:
            received = forward(onward)
        proj = jnp.dot(own_piece, other.reshape(half, width), preferred_element_type=jnp.float32)
        proj = proj + jnp.einsum(
            "nvd,vdc->nc", own_half, gathered.reshape(n_video, half, width),
            preferred_element_type=jnp.float32,
        )
        proj = proj + jnp.einsum(
            "nvd,vdc->nc", rolled, received.reshape(n_video - 1, half, width),
            preferred_element_type=jnp.float32,
        )
        pooled_parts.append(attend(proj, nframes, size, scale, blocks, inner))
    pooled = jnp.concatenate(pooled_parts, axis=1)
    pooled_all = lax.all_gather(pooled, "video", axis=0, tiled=True)
    rows = pooled_all.shape[0]
    partial_proj = jnp.einsum(
        "rc,ckt->rkt", pooled_all, conn_weight, preferred_element_type=jnp.float32
    )
    clip_rows = lax.psum_scatter(
        partial_proj.astype(jnp.bfloat16), "tensor", scatter_dimension=0, tiled=True
    )
    n_tensor = lax.axis_size("tensor")
    if n_video == n_tensor:
        t = lax.axis_index("tensor")
        pieces = [None] * n_tensor
        for k in range(n_tensor):
            pairs = [(a * n_tensor + b, ((b + k) % n_tensor) * n_tensor + a)
                     for a in range(n_video) for b in range(n_tensor)]
            got = lax.ppermute(clip_rows, ("video", "tensor"), pairs)
            pieces[k] = got
        source = [(v - k) % n_tensor for k in range(n_tensor)]
        stacked = jnp.stack(pieces, axis=0)
        order = jnp.argsort(jnp.stack(source))
        clip_proj = jnp.take(stacked, order, axis=0).reshape(rows, 3, -1).astype(jnp.float32)
    else:
        clip_rows = lax.all_gather(clip_rows, "video", axis=0, tiled=False)
        sub = n_video // n_tensor
        clip_rows = clip_rows.reshape((n_tensor, sub) + clip_rows.shape[1:])
        clip_proj = lax.all_to_all(clip_rows, "tensor", 0, 0, tiled=False)
        clip_proj = jnp.transpose(clip_proj, (0, 2, 3, 1, 4))
        clip_proj = clip_proj.reshape(rows, 3, -1).astype(jnp.float32)
    t_heads = clip_proj.shape[2] // HD
    out_rows = rows // n_video
    start = v * out_rows
    own = lax.dynamic_slice_in_dim(clip_proj[:, 0], start, out_rows, axis=0)
    tquery = rms_norm(own.reshape(out_rows, t_heads, HD)).astype(jnp.bfloat16)
    tkey = rms_norm(clip_proj[:, 1].reshape(rows, t_heads, HD)).astype(jnp.bfloat16)
    tvalue = clip_proj[:, 2].reshape(rows, t_heads, HD).astype(jnp.bfloat16)
    seg_rows = jnp.repeat(video_all, POOL)
    row_frame = jnp.arange(rows, dtype=jnp.int32) // POOL
    own_seg = lax.dynamic_slice_in_dim(seg_rows, start, out_rows)
    own_frame = lax.dynamic_slice_in_dim(row_frame, start, out_rows)
    allowed = (seg_rows[None, :] == own_seg[:, None]) & (row_frame[None, :] <= own_frame[:, None])
    logits = jnp.einsum("rhd,khd->hrk", tquery, tkey, preferred_element_type=jnp.float32) * scale
    weights = jnp.where(allowed[None], jnp.exp(logits), jnp.float32(0.0))
    numer = jnp.einsum(
        "hrk,khd->rhd", weights.astype(jnp.bfloat16), tvalue, preferred_element_type=jnp.float32
    )
    denom = jnp.sum(weights, axis=-1)
    summary = numer / jnp.transpose(denom)[:, :, None]
    return summary.reshape(out_rows, t_heads * HD).astype(jnp.bfloat16)


def solution(mesh):
    return jax.shard_map(
        per_device,
        mesh=mesh,
        in_specs=(
            P(("groups", "video"), None, None),
            P(("groups", "video")),
            P("video", None, "tensor"),
            P("tensor", None, "video"),
        ),
        out_specs=P(("groups", "video"), "tensor"),
        check_vma=False,
    )
```

```python
import math

import jax
import jax.numpy as jnp
from jax import lax
from jax.sharding import PartitionSpec as P

HD = 128
PATCH = 256
POOL = 16


def rms_norm(values):
    return values * lax.rsqrt(jnp.mean(values * values, axis=-1, keepdims=True) + 1e-06)


def head_chunks(heads):
    if heads >= 4 and heads % 2 == 0:
        return [1] + [2] * ((heads - 2) // 2) + [1]
    return [1] * heads


def moved_weights(chunk, n_video, after=None):
    v = lax.axis_index("video")
    g = lax.axis_index("groups")
    half = chunk.shape[0] // 2
    mine = lax.dynamic_slice_in_dim(chunk, g * half, half, axis=0)
    if after is not None:
        mine, after = lax.optimization_barrier((mine, after))
    other = lax.dynamic_slice_in_dim(chunk, (1 - g) * half, half, axis=0)
    gathered = lax.all_gather(mine, "video", axis=0, tiled=False)
    onward = jnp.stack(
        [lax.dynamic_index_in_dim(gathered, (v + 1 + i) % n_video, axis=0, keepdims=False)
         for i in range(n_video - 1)]
    )
    return [other, gathered, onward], after


def forward(onward):
    return lax.ppermute(onward, "groups", [(0, 1), (1, 0)])


def attend(proj, nframes, heads, scale, blocks, inner):
    proj = proj.reshape(nframes, PATCH, 3, heads, HD)
    query = rms_norm(proj[:, :, 0]).astype(jnp.bfloat16)
    keys = rms_norm(proj[:, :, 1]).astype(jnp.bfloat16)
    values = proj[:, :, 2].astype(jnp.bfloat16)
    scores = jnp.einsum("fphd,fkhd->fhpk", query, keys, preferred_element_type=jnp.float32) * scale
    probs = jnp.exp(scores)
    probs = (probs / jnp.sum(probs, axis=-1, keepdims=True)).astype(jnp.bfloat16)
    attended = jnp.einsum("fhpk,fkhd->fphd", probs, values, preferred_element_type=jnp.float32)
    grid = attended.reshape(nframes, blocks, inner, blocks, inner, heads, HD)
    return jnp.mean(grid, axis=(2, 4)).reshape(nframes * POOL, heads * HD).astype(jnp.bfloat16)


def per_device(frames, frame_video, qkv_weight, conn_weight):
    scale = 1.0 / math.sqrt(HD)
    blocks = math.isqrt(POOL)
    inner = math.isqrt(PATCH) // blocks
    nframes = frames.shape[0]
    patch_rows = nframes * PATCH
    n_video = lax.axis_size("video")
    assert lax.axis_size("groups") == 2
    v = lax.axis_index("video")
    g = lax.axis_index("groups")
    heads_local = qkv_weight.shape[2] // HD
    sizes = head_chunks(heads_local)
    moved = []
    first = 0
    for size in sizes:
        chunk = qkv_weight[:, :, first * HD:(first + size) * HD]
        first += size
        if len(moved) == len(sizes) - 1 and len(sizes) > 2:
            whole_rows, moved[-1][1] = lax.optimization_barrier((chunk, moved[-1][1]))
            step = [lax.all_gather(whole_rows, "video", axis=0, tiled=True), None, None]
        elif moved:
            step, moved[-1][1] = moved_weights(chunk, n_video, after=moved[-1][1])
        else:
            step, _ = moved_weights(chunk, n_video)
            step.append(forward(step[2]))
        moved.append(step)
    wide = frames.astype(jnp.float32)
    center = wide - jnp.mean(wide, axis=-1, keepdims=True)
    normed = center * lax.rsqrt(jnp.mean(center * center, axis=-1, keepdims=True) + 1e-06)
    normed = normed.astype(jnp.bfloat16).reshape(patch_rows, frames.shape[2])
    local_rows = qkv_weight.shape[0]
    half = local_rows // 2

    def columns(shard, which):
        return lax.dynamic_slice_in_dim(normed, shard * local_rows + which * half, half, axis=1)

    own_half = jnp.stack([columns(u, g) for u in range(n_video)], axis=1)
    own_piece = columns(v, 1 - g)
    rolled = jnp.stack([columns((v + 1 + i) % n_video, 1 - g) for i in range(n_video - 1)], axis=1)
    video_all = lax.all_gather(frame_video, "video", axis=0, tiled=True)
    pooled_parts = []
    for index, size in enumerate(sizes):
        width = 3 * size * HD
        if moved[index][1] is None:
            full = moved[index][0].reshape(n_video * 2 * half, width)
            proj = jnp.dot(normed, full, preferred_element_type=jnp.float32)
            pooled_parts.append(attend(proj, nframes, size, scale, blocks, inner))
            continue
        other, gathered, onward = moved[index][:3]
        if index == 0:
            received = moved[index][3]
            video_all, received = lax.optimization_barrier((video_all, received))
        else:
            received = forward(onward)
        proj = jnp.dot(own_piece, other.reshape(half, width), preferred_element_type=jnp.float32)
        proj = proj + jnp.einsum(
            "nvd,vdc->nc", own_half, gathered.reshape(n_video, half, width),
            preferred_element_type=jnp.float32,
        )
        proj = proj + jnp.einsum(
            "nvd,vdc->nc", rolled, received.reshape(n_video - 1, half, width),
            preferred_element_type=jnp.float32,
        )
        pooled_parts.append(attend(proj, nframes, size, scale, blocks, inner))
    pooled = jnp.concatenate(pooled_parts, axis=1)
    pooled_all = lax.all_gather(pooled, "video", axis=0, tiled=True)
    rows = pooled_all.shape[0]
    partial_proj = jnp.einsum(
        "rc,ckt->rkt", pooled_all, conn_weight, preferred_element_type=jnp.float32
    )
    clip_rows = lax.psum_scatter(
        partial_proj.astype(jnp.bfloat16), "tensor", scatter_dimension=0, tiled=True
    )
    n_tensor = lax.axis_size("tensor")
    if n_video == n_tensor:
        t = lax.axis_index("tensor")
        pieces = [None] * n_tensor
        for k in range(n_tensor):
            pairs = [(a * n_tensor + b, ((b + k) % n_tensor) * n_tensor + a)
                     for a in range(n_video) for b in range(n_tensor)]
            got = lax.ppermute(clip_rows, ("video", "tensor"), pairs)
            pieces[k] = got
        source = [(v - k) % n_tensor for k in range(n_tensor)]
        stacked = jnp.stack(pieces, axis=0)
        order = jnp.argsort(jnp.stack(source))
        clip_proj = jnp.take(stacked, order, axis=0).reshape(rows, 3, -1).astype(jnp.float32)
    else:
        clip_rows = lax.all_gather(clip_rows, "video", axis=0, tiled=False)
        sub = n_video // n_tensor
        clip_rows = clip_rows.reshape((n_tensor, sub) + clip_rows.shape[1:])
        clip_proj = lax.all_to_all(clip_rows, "tensor", 0, 0, tiled=False)
        clip_proj = jnp.transpose(clip_proj, (0, 2, 3, 1, 4))
        clip_proj = clip_proj.reshape(rows, 3, -1).astype(jnp.float32)
    t_heads = clip_proj.shape[2] // HD
    out_rows = rows // n_video
    start = v * out_rows
    own = lax.dynamic_slice_in_dim(clip_proj[:, 0], start, out_rows, axis=0)
    tquery = rms_norm(own.reshape(out_rows, t_heads, HD)).astype(jnp.bfloat16)
    tkey = rms_norm(clip_proj[:, 1].reshape(rows, t_heads, HD)).astype(jnp.bfloat16)
    tvalue = clip_proj[:, 2].reshape(rows, t_heads, HD).astype(jnp.bfloat16)
    seg_rows = jnp.repeat(video_all, POOL)
    row_frame = jnp.arange(rows, dtype=jnp.int32) // POOL
    own_seg = lax.dynamic_slice_in_dim(seg_rows, start, out_rows)
    own_frame = lax.dynamic_slice_in_dim(row_frame, start, out_rows)
    allowed = (seg_rows[None, :] == own_seg[:, None]) & (row_frame[None, :] <= own_frame[:, None])
    logits = jnp.einsum("rhd,khd->hrk", tquery, tkey, preferred_element_type=jnp.float32) * scale
    weights = jnp.where(allowed[None], jnp.exp(logits), jnp.float32(0.0))
    numer = jnp.einsum(
        "hrk,khd->rhd", weights.astype(jnp.bfloat16), tvalue, preferred_element_type=jnp.float32
    )
    denom = jnp.sum(weights, axis=-1)
    summary = numer / jnp.transpose(denom)[:, :, None]
    return summary.reshape(out_rows, t_heads * HD).astype(jnp.bfloat16)


def solution(mesh):
    return jax.shard_map(
        per_device,
        mesh=mesh,
        in_specs=(
            P(("groups", "video"), None, None),
            P(("groups", "video")),
            P("video", None, "tensor"),
            P("tensor", None, "video"),
        ),
        out_specs=P(("groups", "video"), "tensor"),
        check_vma=False,
    )
```

```python
import math

import jax
import jax.numpy as jnp
from jax import lax
from jax.sharding import PartitionSpec as P

HD = 128
PATCH = 256
POOL = 16


def rms_norm(values):
    return values * lax.rsqrt(jnp.mean(values * values, axis=-1, keepdims=True) + 1e-06)


def head_chunks(heads):
    if heads >= 4 and heads % 2 == 0:
        return [1] + [2] * ((heads - 2) // 2) + [1]
    return [1] * heads


def moved_weights(chunk, n_video, after=None):
    v = lax.axis_index("video")
    g = lax.axis_index("groups")
    half = chunk.shape[0] // 2
    mine = lax.dynamic_slice_in_dim(chunk, g * half, half, axis=0)
    if after is not None:
        mine, after = lax.optimization_barrier((mine, after))
    other = lax.dynamic_slice_in_dim(chunk, (1 - g) * half, half, axis=0)
    gathered = lax.all_gather(mine, "video", axis=0, tiled=False)
    onward = jnp.stack(
        [lax.dynamic_index_in_dim(gathered, (v + 1 + i) % n_video, axis=0, keepdims=False)
         for i in range(n_video - 1)]
    )
    return [other, gathered, onward], after


def forward(onward):
    return lax.ppermute(onward, "groups", [(0, 1), (1, 0)])


def attend(proj, nframes, heads, scale, blocks, inner):
    proj = proj.reshape(nframes, PATCH, 3, heads, HD)
    query = rms_norm(proj[:, :, 0]).astype(jnp.bfloat16)
    keys = rms_norm(proj[:, :, 1]).astype(jnp.bfloat16)
    values = proj[:, :, 2].astype(jnp.bfloat16)
    scores = jnp.einsum("fphd,fkhd->fhpk", query, keys, preferred_element_type=jnp.float32) * scale
    probs = jnp.exp(scores)
    probs = (probs / jnp.sum(probs, axis=-1, keepdims=True)).astype(jnp.bfloat16)
    attended = jnp.einsum("fhpk,fkhd->fphd", probs, values, preferred_element_type=jnp.float32)
    grid = attended.reshape(nframes, blocks, inner, blocks, inner, heads, HD)
    return jnp.mean(grid, axis=(2, 4)).reshape(nframes * POOL, heads * HD).astype(jnp.bfloat16)


def per_device(frames, frame_video, qkv_weight, conn_weight):
    scale = 1.0 / math.sqrt(HD)
    blocks = math.isqrt(POOL)
    inner = math.isqrt(PATCH) // blocks
    nframes = frames.shape[0]
    patch_rows = nframes * PATCH
    n_video = lax.axis_size("video")
    assert lax.axis_size("groups") == 2
    v = lax.axis_index("video")
    g = lax.axis_index("groups")
    heads_local = qkv_weight.shape[2] // HD
    sizes = head_chunks(heads_local)
    moved = []
    first = 0
    for index, size in enumerate(sizes):
        chunk = qkv_weight[:, :, first * HD:(first + size) * HD]
        first += size
        after = None
        if index >= 1:
            after = [moved[index - 1][1]]
            if index >= 2 and moved[index - 2][3] is not None:
                after.append(moved[index - 2][3])
        if index == len(sizes) - 1 and len(sizes) > 2:
            whole_rows, after = lax.optimization_barrier((chunk, after))
            step = [lax.all_gather(whole_rows, "video", axis=0, tiled=True), None, None, None]
        else:
            step, after = moved_weights(chunk, n_video, after=after)
            step.append(forward(step[2]))
        if after is not None:
            moved[index - 1][1] = after[0]
            if len(after) > 1:
                moved[index - 2][3] = after[1]
        moved.append(step)
    wide = frames.astype(jnp.float32)
    center = wide - jnp.mean(wide, axis=-1, keepdims=True)
    normed = center * lax.rsqrt(jnp.mean(center * center, axis=-1, keepdims=True) + 1e-06)
    normed = normed.astype(jnp.bfloat16).reshape(patch_rows, frames.shape[2])
    local_rows = qkv_weight.shape[0]
    half = local_rows // 2

    def columns(shard, which):
        return lax.dynamic_slice_in_dim(normed, shard * local_rows + which * half, half, axis=1)

    own_half = jnp.stack([columns(u, g) for u in range(n_video)], axis=1)
    own_piece = columns(v, 1 - g)
    rolled = jnp.stack([columns((v + 1 + i) % n_video, 1 - g) for i in range(n_video - 1)], axis=1)
    video_all = lax.all_gather(frame_video, "video", axis=0, tiled=True)
    pooled_parts = []
    for index, size in enumerate(sizes):
        width = 3 * size * HD
        if moved[index][1] is None:
            full = moved[index][0].reshape(n_video * 2 * half, width)
            proj = jnp.dot(normed, full, preferred_element_type=jnp.float32)
            pooled_parts.append(attend(proj, nframes, size, scale, blocks, inner))
            continue
        other, gathered, onward, received = moved[index]
        if index == 0:
            video_all, received = lax.optimization_barrier((video_all, received))
        proj = jnp.dot(own_piece, other.reshape(half, width), preferred_element_type=jnp.float32)
        proj = proj + jnp.einsum(
            "nvd,vdc->nc", own_half, gathered.reshape(n_video, half, width),
            preferred_element_type=jnp.float32,
        )
        proj = proj + jnp.einsum(
            "nvd,vdc->nc", rolled, received.reshape(n_video - 1, half, width),
            preferred_element_type=jnp.float32,
        )
        pooled_parts.append(attend(proj, nframes, size, scale, blocks, inner))
    pooled = jnp.concatenate(pooled_parts, axis=1)
    pooled_all = lax.all_gather(pooled, "video", axis=0, tiled=True)
    rows = pooled_all.shape[0]
    partial_proj = jnp.einsum(
        "rc,ckt->rkt", pooled_all, conn_weight, preferred_element_type=jnp.float32
    )
    clip_rows = lax.psum_scatter(
        partial_proj.astype(jnp.bfloat16), "tensor", scatter_dimension=0, tiled=True
    )
    n_tensor = lax.axis_size("tensor")
    if n_video == n_tensor:
        t = lax.axis_index("tensor")
        pieces = [None] * n_tensor
        for k in range(n_tensor):
            pairs = [(a * n_tensor + b, ((b + k) % n_tensor) * n_tensor + a)
                     for a in range(n_video) for b in range(n_tensor)]
            got = lax.ppermute(clip_rows, ("video", "tensor"), pairs)
            pieces[k] = got
        source = [(v - k) % n_tensor for k in range(n_tensor)]
        stacked = jnp.stack(pieces, axis=0)
        order = jnp.argsort(jnp.stack(source))
        clip_proj = jnp.take(stacked, order, axis=0).reshape(rows, 3, -1).astype(jnp.float32)
    else:
        clip_rows = lax.all_gather(clip_rows, "video", axis=0, tiled=False)
        sub = n_video // n_tensor
        clip_rows = clip_rows.reshape((n_tensor, sub) + clip_rows.shape[1:])
        clip_proj = lax.all_to_all(clip_rows, "tensor", 0, 0, tiled=False)
        clip_proj = jnp.transpose(clip_proj, (0, 2, 3, 1, 4))
        clip_proj = clip_proj.reshape(rows, 3, -1).astype(jnp.float32)
    t_heads = clip_proj.shape[2] // HD
    out_rows = rows // n_video
    start = v * out_rows
    own = lax.dynamic_slice_in_dim(clip_proj[:, 0], start, out_rows, axis=0)
    tquery = rms_norm(own.reshape(out_rows, t_heads, HD)).astype(jnp.bfloat16)
    tkey = rms_norm(clip_proj[:, 1].reshape(rows, t_heads, HD)).astype(jnp.bfloat16)
    tvalue = clip_proj[:, 2].reshape(rows, t_heads, HD).astype(jnp.bfloat16)
    seg_rows = jnp.repeat(video_all, POOL)
    row_frame = jnp.arange(rows, dtype=jnp.int32) // POOL
    own_seg = lax.dynamic_slice_in_dim(seg_rows, start, out_rows)
    own_frame = lax.dynamic_slice_in_dim(row_frame, start, out_rows)
    allowed = (seg_rows[None, :] == own_seg[:, None]) & (row_frame[None, :] <= own_frame[:, None])
    logits = jnp.einsum("rhd,khd->hrk", tquery, tkey, preferred_element_type=jnp.float32) * scale
    weights = jnp.where(allowed[None], jnp.exp(logits), jnp.float32(0.0))
    numer = jnp.einsum(
        "hrk,khd->rhd", weights.astype(jnp.bfloat16), tvalue, preferred_element_type=jnp.float32
    )
    denom = jnp.sum(weights, axis=-1)
    summary = numer / jnp.transpose(denom)[:, :, None]
    return summary.reshape(out_rows, t_heads * HD).astype(jnp.bfloat16)


def solution(mesh):
    return jax.shard_map(
        per_device,
        mesh=mesh,
        in_specs=(
            P(("groups", "video"), None, None),
            P(("groups", "video")),
            P("video", None, "tensor"),
            P("tensor", None, "video"),
        ),
        out_specs=P(("groups", "video"), "tensor"),
        check_vma=False,
    )
```

```python
import math

import jax
import jax.numpy as jnp
from jax import lax
from jax.sharding import PartitionSpec as P

HD = 128
PATCH = 256
POOL = 16


def rms_norm(values):
    return values * lax.rsqrt(jnp.mean(values * values, axis=-1, keepdims=True) + 1e-06)


def head_chunks(heads):
    if heads >= 4 and heads % 2 == 0:
        return [2] * ((heads - 2) // 2) + [1, 1]
    return [1] * heads


def moved_weights(chunk, n_video, after=None):
    v = lax.axis_index("video")
    g = lax.axis_index("groups")
    half = chunk.shape[0] // 2
    mine = lax.dynamic_slice_in_dim(chunk, g * half, half, axis=0)
    if after is not None:
        mine, after = lax.optimization_barrier((mine, after))
    other = lax.dynamic_slice_in_dim(chunk, (1 - g) * half, half, axis=0)
    gathered = lax.all_gather(mine, "video", axis=0, tiled=False)
    onward = jnp.stack(
        [lax.dynamic_index_in_dim(gathered, (v + 1 + i) % n_video, axis=0, keepdims=False)
         for i in range(n_video - 1)]
    )
    return [other, gathered, onward], after


def forward(onward):
    return lax.ppermute(onward, "groups", [(0, 1), (1, 0)])


def attend(proj, nframes, heads, scale, blocks, inner):
    proj = proj.reshape(nframes, PATCH, 3, heads, HD)
    query = rms_norm(proj[:, :, 0]).astype(jnp.bfloat16)
    keys = rms_norm(proj[:, :, 1]).astype(jnp.bfloat16)
    values = proj[:, :, 2].astype(jnp.bfloat16)
    scores = jnp.einsum("fphd,fkhd->fhpk", query, keys, preferred_element_type=jnp.float32) * scale
    probs = jnp.exp(scores)
    probs = (probs / jnp.sum(probs, axis=-1, keepdims=True)).astype(jnp.bfloat16)
    attended = jnp.einsum("fhpk,fkhd->fphd", probs, values, preferred_element_type=jnp.float32)
    grid = attended.reshape(nframes, blocks, inner, blocks, inner, heads, HD)
    return jnp.mean(grid, axis=(2, 4)).reshape(nframes * POOL, heads * HD).astype(jnp.bfloat16)


def per_device(frames, frame_video, qkv_weight, conn_weight):
    scale = 1.0 / math.sqrt(HD)
    blocks = math.isqrt(POOL)
    inner = math.isqrt(PATCH) // blocks
    nframes = frames.shape[0]
    patch_rows = nframes * PATCH
    n_video = lax.axis_size("video")
    assert lax.axis_size("groups") == 2
    v = lax.axis_index("video")
    g = lax.axis_index("groups")
    heads_local = qkv_weight.shape[2] // HD
    sizes = head_chunks(heads_local)
    moved = []
    first = 0
    for size in sizes:
        chunk = qkv_weight[:, :, first * HD:(first + size) * HD]
        first += size
        if len(moved) == len(sizes) - 1 and len(sizes) > 2:
            whole_rows, moved[-1][1] = lax.optimization_barrier((chunk, moved[-1][1]))
            step = [lax.all_gather(whole_rows, "video", axis=0, tiled=True), None, None]
        elif moved:
            step, moved[-1][1] = moved_weights(chunk, n_video, after=moved[-1][1])
        else:
            step, _ = moved_weights(chunk, n_video)
            step.append(forward(step[2]))
        moved.append(step)
    wide = frames.astype(jnp.float32)
    center = wide - jnp.mean(wide, axis=-1, keepdims=True)
    normed = center * lax.rsqrt(jnp.mean(center * center, axis=-1, keepdims=True) + 1e-06)
    normed = normed.astype(jnp.bfloat16).reshape(patch_rows, frames.shape[2])
    local_rows = qkv_weight.shape[0]
    half = local_rows // 2

    def columns(shard, which):
        return lax.dynamic_slice_in_dim(normed, shard * local_rows + which * half, half, axis=1)

    own_half = jnp.stack([columns(u, g) for u in range(n_video)], axis=1)
    own_piece = columns(v, 1 - g)
    rolled = jnp.stack([columns((v + 1 + i) % n_video, 1 - g) for i in range(n_video - 1)], axis=1)
    video_all = lax.all_gather(frame_video, "video", axis=0, tiled=True)
    pooled_parts = []
    for index, size in enumerate(sizes):
        width = 3 * size * HD
        if moved[index][1] is None:
            full = moved[index][0].reshape(n_video * 2 * half, width)
            proj = jnp.dot(normed, full, preferred_element_type=jnp.float32)
            pooled_parts.append(attend(proj, nframes, size, scale, blocks, inner))
            continue
        other, gathered, onward = moved[index][:3]
        if index == 0:
            received = moved[index][3]
            video_all, received = lax.optimization_barrier((video_all, received))
        else:
            received = forward(onward)
        proj = jnp.dot(own_piece, other.reshape(half, width), preferred_element_type=jnp.float32)
        proj = proj + jnp.einsum(
            "nvd,vdc->nc", own_half, gathered.reshape(n_video, half, width),
            preferred_element_type=jnp.float32,
        )
        proj = proj + jnp.einsum(
            "nvd,vdc->nc", rolled, received.reshape(n_video - 1, half, width),
            preferred_element_type=jnp.float32,
        )
        pooled_parts.append(attend(proj, nframes, size, scale, blocks, inner))
    pooled = jnp.concatenate(pooled_parts, axis=1)
    pooled_all = lax.all_gather(pooled, "video", axis=0, tiled=True)
    rows = pooled_all.shape[0]
    partial_proj = jnp.einsum(
        "rc,ckt->rkt", pooled_all, conn_weight, preferred_element_type=jnp.float32
    )
    clip_rows = lax.psum_scatter(
        partial_proj.astype(jnp.bfloat16), "tensor", scatter_dimension=0, tiled=True
    )
    n_tensor = lax.axis_size("tensor")
    if n_video == n_tensor:
        t = lax.axis_index("tensor")
        pieces = [None] * n_tensor
        for k in range(n_tensor):
            pairs = [(a * n_tensor + b, ((b + k) % n_tensor) * n_tensor + a)
                     for a in range(n_video) for b in range(n_tensor)]
            got = lax.ppermute(clip_rows, ("video", "tensor"), pairs)
            pieces[k] = got
        source = [(v - k) % n_tensor for k in range(n_tensor)]
        stacked = jnp.stack(pieces, axis=0)
        order = jnp.argsort(jnp.stack(source))
        clip_proj = jnp.take(stacked, order, axis=0).reshape(rows, 3, -1).astype(jnp.float32)
    else:
        clip_rows = lax.all_gather(clip_rows, "video", axis=0, tiled=False)
        sub = n_video // n_tensor
        clip_rows = clip_rows.reshape((n_tensor, sub) + clip_rows.shape[1:])
        clip_proj = lax.all_to_all(clip_rows, "tensor", 0, 0, tiled=False)
        clip_proj = jnp.transpose(clip_proj, (0, 2, 3, 1, 4))
        clip_proj = clip_proj.reshape(rows, 3, -1).astype(jnp.float32)
    t_heads = clip_proj.shape[2] // HD
    out_rows = rows // n_video
    start = v * out_rows
    own = lax.dynamic_slice_in_dim(clip_proj[:, 0], start, out_rows, axis=0)
    tquery = rms_norm(own.reshape(out_rows, t_heads, HD)).astype(jnp.bfloat16)
    tkey = rms_norm(clip_proj[:, 1].reshape(rows, t_heads, HD)).astype(jnp.bfloat16)
    tvalue = clip_proj[:, 2].reshape(rows, t_heads, HD).astype(jnp.bfloat16)
    seg_rows = jnp.repeat(video_all, POOL)
    row_frame = jnp.arange(rows, dtype=jnp.int32) // POOL
    own_seg = lax.dynamic_slice_in_dim(seg_rows, start, out_rows)
    own_frame = lax.dynamic_slice_in_dim(row_frame, start, out_rows)
    allowed = (seg_rows[None, :] == own_seg[:, None]) & (row_frame[None, :] <= own_frame[:, None])
    logits = jnp.einsum("rhd,khd->hrk", tquery, tkey, preferred_element_type=jnp.float32) * scale
    weights = jnp.where(allowed[None], jnp.exp(logits), jnp.float32(0.0))
    numer = jnp.einsum(
        "hrk,khd->rhd", weights.astype(jnp.bfloat16), tvalue, preferred_element_type=jnp.float32
    )
    denom = jnp.sum(weights, axis=-1)
    summary = numer / jnp.transpose(denom)[:, :, None]
    return summary.reshape(out_rows, t_heads * HD).astype(jnp.bfloat16)


def solution(mesh):
    return jax.shard_map(
        per_device,
        mesh=mesh,
        in_specs=(
            P(("groups", "video"), None, None),
            P(("groups", "video")),
            P("video", None, "tensor"),
            P("tensor", None, "video"),
        ),
        out_specs=P(("groups", "video"), "tensor"),
        check_vma=False,
    )
```

```python
import math

import jax
import jax.numpy as jnp
from jax import lax
from jax.sharding import PartitionSpec as P

HD = 128
PATCH = 256
POOL = 16


def rms_norm(values):
    return values * lax.rsqrt(jnp.mean(values * values, axis=-1, keepdims=True) + 1e-06)


def head_chunks(heads):
    if heads >= 4 and heads % 2 == 0:
        return [1] + [2] * ((heads - 2) // 2) + [1]
    return [1] * heads


def moved_weights(chunk, n_video, after=None):
    v = lax.axis_index("video")
    g = lax.axis_index("groups")
    half = chunk.shape[0] // 2
    mine = lax.dynamic_slice_in_dim(chunk, g * half, half, axis=0)
    if after is not None:
        mine, after = lax.optimization_barrier((mine, after))
    other = lax.dynamic_slice_in_dim(chunk, (1 - g) * half, half, axis=0)
    gathered = lax.all_gather(mine, "video", axis=0, tiled=True)
    onward = jnp.concatenate(
        [lax.dynamic_slice_in_dim(gathered, ((v + 1 + i) % n_video) * half, half, axis=0)
         for i in range(n_video - 1)], axis=0
    )
    return [other, gathered, onward], after


def forward(onward):
    return lax.ppermute(onward, "groups", [(0, 1), (1, 0)])


def attend(proj, nframes, heads, scale, blocks, inner):
    proj = proj.reshape(nframes, PATCH, 3, heads, HD)
    query = rms_norm(proj[:, :, 0]).astype(jnp.bfloat16)
    keys = rms_norm(proj[:, :, 1]).astype(jnp.bfloat16)
    values = proj[:, :, 2].astype(jnp.bfloat16)
    scores = jnp.einsum("fphd,fkhd->fhpk", query, keys, preferred_element_type=jnp.float32) * scale
    probs = jnp.exp(scores)
    probs = (probs / jnp.sum(probs, axis=-1, keepdims=True)).astype(jnp.bfloat16)
    attended = jnp.einsum("fhpk,fkhd->fphd", probs, values, preferred_element_type=jnp.float32)
    grid = attended.reshape(nframes, blocks, inner, blocks, inner, heads, HD)
    return jnp.mean(grid, axis=(2, 4)).reshape(nframes * POOL, heads * HD).astype(jnp.bfloat16)


def per_device(frames, frame_video, qkv_weight, conn_weight):
    scale = 1.0 / math.sqrt(HD)
    blocks = math.isqrt(POOL)
    inner = math.isqrt(PATCH) // blocks
    nframes = frames.shape[0]
    patch_rows = nframes * PATCH
    n_video = lax.axis_size("video")
    assert lax.axis_size("groups") == 2
    v = lax.axis_index("video")
    g = lax.axis_index("groups")
    heads_local = qkv_weight.shape[2] // HD
    sizes = head_chunks(heads_local)
    moved = []
    first = 0
    for size in sizes:
        chunk = qkv_weight[:, :, first * HD:(first + size) * HD]
        first += size
        if len(moved) == len(sizes) - 1 and len(sizes) > 2:
            whole_rows, moved[-1][1] = lax.optimization_barrier((chunk, moved[-1][1]))
            step = [lax.all_gather(whole_rows, "video", axis=0, tiled=True), None, None]
        elif moved:
            step, moved[-1][1] = moved_weights(chunk, n_video, after=moved[-1][1])
        else:
            step, _ = moved_weights(chunk, n_video)
            step.append(forward(step[2]))
        moved.append(step)
    wide = frames.astype(jnp.float32)
    center = wide - jnp.mean(wide, axis=-1, keepdims=True)
    normed = center * lax.rsqrt(jnp.mean(center * center, axis=-1, keepdims=True) + 1e-06)
    normed = normed.astype(jnp.bfloat16).reshape(patch_rows, frames.shape[2])
    local_rows = qkv_weight.shape[0]
    half = local_rows // 2

    def columns(shard, which):
        return lax.dynamic_slice_in_dim(normed, shard * local_rows + which * half, half, axis=1)

    own_half = jnp.concatenate([columns(u, g) for u in range(n_video)], axis=1)
    own_piece = columns(v, 1 - g)
    rolled = jnp.concatenate(
        [columns((v + 1 + i) % n_video, 1 - g) for i in range(n_video - 1)], axis=1
    )
    video_all = lax.all_gather(frame_video, "video", axis=0, tiled=True)
    pooled_parts = []
    for index, size in enumerate(sizes):
        width = 3 * size * HD
        if moved[index][1] is None:
            full = moved[index][0].reshape(n_video * 2 * half, width)
            proj = jnp.dot(normed, full, preferred_element_type=jnp.float32)
            pooled_parts.append(attend(proj, nframes, size, scale, blocks, inner))
            continue
        other, gathered, onward = moved[index][:3]
        if index == 0:
            received = moved[index][3]
            video_all, received = lax.optimization_barrier((video_all, received))
        else:
            received = forward(onward)
        proj = jnp.dot(own_piece, other.reshape(half, width), preferred_element_type=jnp.float32)
        proj = proj + jnp.dot(
            own_half, gathered.reshape(n_video * half, width), preferred_element_type=jnp.float32
        )
        proj = proj + jnp.dot(
            rolled, received.reshape((n_video - 1) * half, width),
            preferred_element_type=jnp.float32,
        )
        pooled_parts.append(attend(proj, nframes, size, scale, blocks, inner))
    pooled = jnp.concatenate(pooled_parts, axis=1)
    pooled_all = lax.all_gather(pooled, "video", axis=0, tiled=True)
    rows = pooled_all.shape[0]
    partial_proj = jnp.einsum(
        "rc,ckt->rkt", pooled_all, conn_weight, preferred_element_type=jnp.float32
    )
    clip_rows = lax.psum_scatter(
        partial_proj.astype(jnp.bfloat16), "tensor", scatter_dimension=0, tiled=True
    )
    n_tensor = lax.axis_size("tensor")
    if n_video == n_tensor:
        t = lax.axis_index("tensor")
        pieces = [None] * n_tensor
        for k in range(n_tensor):
            pairs = [(a * n_tensor + b, ((b + k) % n_tensor) * n_tensor + a)
                     for a in range(n_video) for b in range(n_tensor)]
            got = lax.ppermute(clip_rows, ("video", "tensor"), pairs)
            pieces[k] = got
        source = [(v - k) % n_tensor for k in range(n_tensor)]
        stacked = jnp.stack(pieces, axis=0)
        order = jnp.argsort(jnp.stack(source))
        clip_proj = jnp.take(stacked, order, axis=0).reshape(rows, 3, -1).astype(jnp.float32)
    else:
        clip_rows = lax.all_gather(clip_rows, "video", axis=0, tiled=False)
        sub = n_video // n_tensor
        clip_rows = clip_rows.reshape((n_tensor, sub) + clip_rows.shape[1:])
        clip_proj = lax.all_to_all(clip_rows, "tensor", 0, 0, tiled=False)
        clip_proj = jnp.transpose(clip_proj, (0, 2, 3, 1, 4))
        clip_proj = clip_proj.reshape(rows, 3, -1).astype(jnp.float32)
    t_heads = clip_proj.shape[2] // HD
    out_rows = rows // n_video
    start = v * out_rows
    own = lax.dynamic_slice_in_dim(clip_proj[:, 0], start, out_rows, axis=0)
    tquery = rms_norm(own.reshape(out_rows, t_heads, HD)).astype(jnp.bfloat16)
    tkey = rms_norm(clip_proj[:, 1].reshape(rows, t_heads, HD)).astype(jnp.bfloat16)
    tvalue = clip_proj[:, 2].reshape(rows, t_heads, HD).astype(jnp.bfloat16)
    seg_rows = jnp.repeat(video_all, POOL)
    row_frame = jnp.arange(rows, dtype=jnp.int32) // POOL
    own_seg = lax.dynamic_slice_in_dim(seg_rows, start, out_rows)
    own_frame = lax.dynamic_slice_in_dim(row_frame, start, out_rows)
    allowed = (seg_rows[None, :] == own_seg[:, None]) & (row_frame[None, :] <= own_frame[:, None])
    logits = jnp.einsum("rhd,khd->hrk", tquery, tkey, preferred_element_type=jnp.float32) * scale
    weights = jnp.where(allowed[None], jnp.exp(logits), jnp.float32(0.0))
    numer = jnp.einsum(
        "hrk,khd->rhd", weights.astype(jnp.bfloat16), tvalue, preferred_element_type=jnp.float32
    )
    denom = jnp.sum(weights, axis=-1)
    summary = numer / jnp.transpose(denom)[:, :, None]
    return summary.reshape(out_rows, t_heads * HD).astype(jnp.bfloat16)


def solution(mesh):
    return jax.shard_map(
        per_device,
        mesh=mesh,
        in_specs=(
            P(("groups", "video"), None, None),
            P(("groups", "video")),
            P("video", None, "tensor"),
            P("tensor", None, "video"),
        ),
        out_specs=P(("groups", "video"), "tensor"),
        check_vma=False,
    )
```

```python
import math

import jax
import jax.numpy as jnp
from jax import lax
from jax.sharding import PartitionSpec as P

HD = 128
PATCH = 256
POOL = 16


def rms_norm(values):
    return values * lax.rsqrt(jnp.mean(values * values, axis=-1, keepdims=True) + 1e-06)


def head_chunks(heads):
    if heads >= 4 and heads % 2 == 0:
        return [1] + [2] * ((heads - 2) // 2) + [1]
    return [1] * heads


def moved_weights(chunk, n_video, after=None):
    v = lax.axis_index("video")
    g = lax.axis_index("groups")
    half = chunk.shape[0] // 2
    mine = lax.dynamic_slice_in_dim(chunk, g * half, half, axis=0)
    if after is not None:
        mine, after = lax.optimization_barrier((mine, after))
    other = lax.dynamic_slice_in_dim(chunk, (1 - g) * half, half, axis=0)
    gathered = lax.all_gather(mine, "video", axis=0, tiled=True)
    onward = jnp.concatenate(
        [lax.dynamic_slice_in_dim(gathered, ((v + 1 + i) % n_video) * half, half, axis=0)
         for i in range(n_video - 1)], axis=0
    )
    return [other, gathered, onward], after


def forward(onward):
    return lax.ppermute(onward, "groups", [(0, 1), (1, 0)])


def attend(proj, nframes, heads, scale, blocks, inner):
    proj = proj.reshape(nframes, PATCH, 3, heads, HD)
    query = rms_norm(proj[:, :, 0]).astype(jnp.bfloat16)
    keys = rms_norm(proj[:, :, 1]).astype(jnp.bfloat16)
    values = proj[:, :, 2].astype(jnp.bfloat16)
    scores = jnp.einsum("fphd,fkhd->fhpk", query, keys, preferred_element_type=jnp.float32) * scale
    probs = jnp.exp(scores)
    probs = (probs / jnp.sum(probs, axis=-1, keepdims=True)).astype(jnp.bfloat16)
    attended = jnp.einsum("fhpk,fkhd->fphd", probs, values, preferred_element_type=jnp.float32)
    grid = attended.reshape(nframes, blocks, inner, blocks, inner, heads, HD)
    return jnp.mean(grid, axis=(2, 4)).reshape(nframes * POOL, heads * HD).astype(jnp.bfloat16)


def per_device(frames, frame_video, qkv_weight, conn_weight):
    scale = 1.0 / math.sqrt(HD)
    blocks = math.isqrt(POOL)
    inner = math.isqrt(PATCH) // blocks
    nframes = frames.shape[0]
    patch_rows = nframes * PATCH
    n_video = lax.axis_size("video")
    assert lax.axis_size("groups") == 2
    v = lax.axis_index("video")
    g = lax.axis_index("groups")
    heads_local = qkv_weight.shape[2] // HD
    sizes = head_chunks(heads_local)
    moved = []
    first = 0
    for size in sizes:
        chunk = qkv_weight[:, :, first * HD:(first + size) * HD]
        first += size
        if len(moved) == len(sizes) - 1 and len(sizes) > 2:
            whole_rows, moved[-1][1] = lax.optimization_barrier((chunk, moved[-1][1]))
            step = [lax.all_gather(whole_rows, "video", axis=0, tiled=True), None, None]
        elif moved:
            step, moved[-1][1] = moved_weights(chunk, n_video, after=moved[-1][1])
        else:
            step, _ = moved_weights(chunk, n_video)
            step.append(forward(step[2]))
            step[3], frames = lax.optimization_barrier((step[3], frames))
        moved.append(step)
    wide = frames.astype(jnp.float32)
    center = wide - jnp.mean(wide, axis=-1, keepdims=True)
    normed = center * lax.rsqrt(jnp.mean(center * center, axis=-1, keepdims=True) + 1e-06)
    normed = normed.astype(jnp.bfloat16).reshape(patch_rows, frames.shape[2])
    local_rows = qkv_weight.shape[0]
    half = local_rows // 2

    def columns(shard, which):
        return lax.dynamic_slice_in_dim(normed, shard * local_rows + which * half, half, axis=1)

    own_half = jnp.concatenate([columns(u, g) for u in range(n_video)], axis=1)
    own_piece = columns(v, 1 - g)
    rolled = jnp.concatenate(
        [columns((v + 1 + i) % n_video, 1 - g) for i in range(n_video - 1)], axis=1
    )
    video_all = lax.all_gather(frame_video, "video", axis=0, tiled=True)
    pooled_parts = []
    for index, size in enumerate(sizes):
        width = 3 * size * HD
        if moved[index][1] is None:
            full = moved[index][0].reshape(n_video * 2 * half, width)
            proj = jnp.dot(normed, full, preferred_element_type=jnp.float32)
            pooled_parts.append(attend(proj, nframes, size, scale, blocks, inner))
            continue
        other, gathered, onward = moved[index][:3]
        if index == 0:
            received = moved[index][3]
            video_all, received = lax.optimization_barrier((video_all, received))
        else:
            received = forward(onward)
        proj = jnp.dot(own_piece, other.reshape(half, width), preferred_element_type=jnp.float32)
        proj = proj + jnp.dot(
            own_half, gathered.reshape(n_video * half, width), preferred_element_type=jnp.float32
        )
        proj = proj + jnp.dot(
            rolled, received.reshape((n_video - 1) * half, width),
            preferred_element_type=jnp.float32,
        )
        pooled_parts.append(attend(proj, nframes, size, scale, blocks, inner))
    pooled = jnp.concatenate(pooled_parts, axis=1)
    pooled_all = lax.all_gather(pooled, "video", axis=0, tiled=True)
    rows = pooled_all.shape[0]
    partial_proj = jnp.einsum(
        "rc,ckt->rkt", pooled_all, conn_weight, preferred_element_type=jnp.float32
    )
    clip_rows = lax.psum_scatter(
        partial_proj.astype(jnp.bfloat16), "tensor", scatter_dimension=0, tiled=True
    )
    n_tensor = lax.axis_size("tensor")
    if n_video == n_tensor:
        t = lax.axis_index("tensor")
        pieces = [None] * n_tensor
        for k in range(n_tensor):
            pairs = [(a * n_tensor + b, ((b + k) % n_tensor) * n_tensor + a)
                     for a in range(n_video) for b in range(n_tensor)]
            got = lax.ppermute(clip_rows, ("video", "tensor"), pairs)
            pieces[k] = got
        source = [(v - k) % n_tensor for k in range(n_tensor)]
        stacked = jnp.stack(pieces, axis=0)
        order = jnp.argsort(jnp.stack(source))
        clip_proj = jnp.take(stacked, order, axis=0).reshape(rows, 3, -1).astype(jnp.float32)
    else:
        clip_rows = lax.all_gather(clip_rows, "video", axis=0, tiled=False)
        sub = n_video // n_tensor
        clip_rows = clip_rows.reshape((n_tensor, sub) + clip_rows.shape[1:])
        clip_proj = lax.all_to_all(clip_rows, "tensor", 0, 0, tiled=False)
        clip_proj = jnp.transpose(clip_proj, (0, 2, 3, 1, 4))
        clip_proj = clip_proj.reshape(rows, 3, -1).astype(jnp.float32)
    t_heads = clip_proj.shape[2] // HD
    out_rows = rows // n_video
    start = v * out_rows
    own = lax.dynamic_slice_in_dim(clip_proj[:, 0], start, out_rows, axis=0)
    tquery = rms_norm(own.reshape(out_rows, t_heads, HD)).astype(jnp.bfloat16)
    tkey = rms_norm(clip_proj[:, 1].reshape(rows, t_heads, HD)).astype(jnp.bfloat16)
    tvalue = clip_proj[:, 2].reshape(rows, t_heads, HD).astype(jnp.bfloat16)
    seg_rows = jnp.repeat(video_all, POOL)
    row_frame = jnp.arange(rows, dtype=jnp.int32) // POOL
    own_seg = lax.dynamic_slice_in_dim(seg_rows, start, out_rows)
    own_frame = lax.dynamic_slice_in_dim(row_frame, start, out_rows)
    allowed = (seg_rows[None, :] == own_seg[:, None]) & (row_frame[None, :] <= own_frame[:, None])
    logits = jnp.einsum("rhd,khd->hrk", tquery, tkey, preferred_element_type=jnp.float32) * scale
    weights = jnp.where(allowed[None], jnp.exp(logits), jnp.float32(0.0))
    numer = jnp.einsum(
        "hrk,khd->rhd", weights.astype(jnp.bfloat16), tvalue, preferred_element_type=jnp.float32
    )
    denom = jnp.sum(weights, axis=-1)
    summary = numer / jnp.transpose(denom)[:, :, None]
    return summary.reshape(out_rows, t_heads * HD).astype(jnp.bfloat16)


def solution(mesh):
    return jax.shard_map(
        per_device,
        mesh=mesh,
        in_specs=(
            P(("groups", "video"), None, None),
            P(("groups", "video")),
            P("video", None, "tensor"),
            P("tensor", None, "video"),
        ),
        out_specs=P(("groups", "video"), "tensor"),
        check_vma=False,
    )
```

```python
import math

import jax
import jax.numpy as jnp
from jax import lax
from jax.sharding import PartitionSpec as P

HD = 128
PATCH = 256
POOL = 16


def rms_norm(values):
    return values * lax.rsqrt(jnp.mean(values * values, axis=-1, keepdims=True) + 1e-06)


def head_chunks(heads):
    if heads >= 4 and heads % 2 == 0:
        return [1] + [2] * ((heads - 2) // 2) + [1]
    return [1] * heads


def moved_weights(chunk, n_video, after=None):
    v = lax.axis_index("video")
    g = lax.axis_index("groups")
    half = chunk.shape[0] // 2
    mine = lax.dynamic_slice_in_dim(chunk, g * half, half, axis=0)
    if after is not None:
        mine, after = lax.optimization_barrier((mine, after))
    other = lax.dynamic_slice_in_dim(chunk, (1 - g) * half, half, axis=0)
    gathered = lax.all_gather(mine, "video", axis=0, tiled=True)
    onward = jnp.concatenate(
        [lax.dynamic_slice_in_dim(gathered, ((v + 1 + i) % n_video) * half, half, axis=0)
         for i in range(n_video - 1)], axis=0
    )
    return [other, gathered, onward], after


def forward(onward):
    return lax.ppermute(onward, "groups", [(0, 1), (1, 0)])


def attend(proj, nframes, heads, scale, blocks, inner):
    proj = proj.reshape(nframes, PATCH, 3, heads, HD)
    query = rms_norm(proj[:, :, 0]).astype(jnp.bfloat16)
    keys = rms_norm(proj[:, :, 1]).astype(jnp.bfloat16)
    values = proj[:, :, 2].astype(jnp.bfloat16)
    scores = jnp.einsum("fphd,fkhd->fhpk", query, keys, preferred_element_type=jnp.float32) * scale
    probs = jnp.exp(scores)
    probs = (probs / jnp.sum(probs, axis=-1, keepdims=True)).astype(jnp.bfloat16)
    attended = jnp.einsum("fhpk,fkhd->fphd", probs, values, preferred_element_type=jnp.float32)
    grid = attended.reshape(nframes, blocks, inner, blocks, inner, heads, HD)
    return jnp.mean(grid, axis=(2, 4)).reshape(nframes * POOL, heads * HD).astype(jnp.bfloat16)


def per_device(frames, frame_video, qkv_weight, conn_weight):
    scale = 1.0 / math.sqrt(HD)
    blocks = math.isqrt(POOL)
    inner = math.isqrt(PATCH) // blocks
    nframes = frames.shape[0]
    patch_rows = nframes * PATCH
    n_video = lax.axis_size("video")
    assert lax.axis_size("groups") == 2
    v = lax.axis_index("video")
    g = lax.axis_index("groups")
    heads_local = qkv_weight.shape[2] // HD
    sizes = head_chunks(heads_local)
    moved = []
    first = 0
    for size in sizes:
        chunk = qkv_weight[:, :, first * HD:(first + size) * HD]
        first += size
        if len(moved) == len(sizes) - 1 and len(sizes) > 2:
            whole_rows, moved[-1][1] = lax.optimization_barrier((chunk, moved[-1][1]))
            step = [lax.all_gather(whole_rows, "video", axis=0, tiled=True), None, None]
        elif moved:
            step, moved[-1][1] = moved_weights(chunk, n_video, after=moved[-1][1])
            step.append(forward(step[2]))
        else:
            step, _ = moved_weights(chunk, n_video)
            step.append(forward(step[2]))
            step[3], frames = lax.optimization_barrier((step[3], frames))
        moved.append(step)
    wide = frames.astype(jnp.float32)
    center = wide - jnp.mean(wide, axis=-1, keepdims=True)
    normed = center * lax.rsqrt(jnp.mean(center * center, axis=-1, keepdims=True) + 1e-06)
    normed = normed.astype(jnp.bfloat16).reshape(patch_rows, frames.shape[2])
    local_rows = qkv_weight.shape[0]
    half = local_rows // 2

    def columns(shard, which):
        return lax.dynamic_slice_in_dim(normed, shard * local_rows + which * half, half, axis=1)

    own_half = jnp.concatenate([columns(u, g) for u in range(n_video)], axis=1)
    own_piece = columns(v, 1 - g)
    rolled = jnp.concatenate(
        [columns((v + 1 + i) % n_video, 1 - g) for i in range(n_video - 1)], axis=1
    )
    if len(moved) > 2 and moved[1][3] is not None:
        moved[1][3], own_half = lax.optimization_barrier((moved[1][3], own_half))
    video_all = lax.all_gather(frame_video, "video", axis=0, tiled=True)
    pooled_parts = []
    for index, size in enumerate(sizes):
        width = 3 * size * HD
        if moved[index][1] is None:
            full = moved[index][0].reshape(n_video * 2 * half, width)
            proj = jnp.dot(normed, full, preferred_element_type=jnp.float32)
            pooled_parts.append(attend(proj, nframes, size, scale, blocks, inner))
            continue
        other, gathered, onward, received = moved[index]
        if index == 0:
            video_all, received = lax.optimization_barrier((video_all, received))
        proj = jnp.dot(own_piece, other.reshape(half, width), preferred_element_type=jnp.float32)
        proj = proj + jnp.dot(
            own_half, gathered.reshape(n_video * half, width), preferred_element_type=jnp.float32
        )
        proj = proj + jnp.dot(
            rolled, received.reshape((n_video - 1) * half, width),
            preferred_element_type=jnp.float32,
        )
        pooled_parts.append(attend(proj, nframes, size, scale, blocks, inner))
    pooled = jnp.concatenate(pooled_parts, axis=1)
    pooled_all = lax.all_gather(pooled, "video", axis=0, tiled=True)
    rows = pooled_all.shape[0]
    partial_proj = jnp.einsum(
        "rc,ckt->rkt", pooled_all, conn_weight, preferred_element_type=jnp.float32
    )
    clip_rows = lax.psum_scatter(
        partial_proj.astype(jnp.bfloat16), "tensor", scatter_dimension=0, tiled=True
    )
    n_tensor = lax.axis_size("tensor")
    if n_video == n_tensor:
        t = lax.axis_index("tensor")
        pieces = [None] * n_tensor
        for k in range(n_tensor):
            pairs = [(a * n_tensor + b, ((b + k) % n_tensor) * n_tensor + a)
                     for a in range(n_video) for b in range(n_tensor)]
            got = lax.ppermute(clip_rows, ("video", "tensor"), pairs)
            pieces[k] = got
        source = [(v - k) % n_tensor for k in range(n_tensor)]
        stacked = jnp.stack(pieces, axis=0)
        order = jnp.argsort(jnp.stack(source))
        clip_proj = jnp.take(stacked, order, axis=0).reshape(rows, 3, -1).astype(jnp.float32)
    else:
        clip_rows = lax.all_gather(clip_rows, "video", axis=0, tiled=False)
        sub = n_video // n_tensor
        clip_rows = clip_rows.reshape((n_tensor, sub) + clip_rows.shape[1:])
        clip_proj = lax.all_to_all(clip_rows, "tensor", 0, 0, tiled=False)
        clip_proj = jnp.transpose(clip_proj, (0, 2, 3, 1, 4))
        clip_proj = clip_proj.reshape(rows, 3, -1).astype(jnp.float32)
    t_heads = clip_proj.shape[2] // HD
    out_rows = rows // n_video
    start = v * out_rows
    own = lax.dynamic_slice_in_dim(clip_proj[:, 0], start, out_rows, axis=0)
    tquery = rms_norm(own.reshape(out_rows, t_heads, HD)).astype(jnp.bfloat16)
    tkey = rms_norm(clip_proj[:, 1].reshape(rows, t_heads, HD)).astype(jnp.bfloat16)
    tvalue = clip_proj[:, 2].reshape(rows, t_heads, HD).astype(jnp.bfloat16)
    seg_rows = jnp.repeat(video_all, POOL)
    row_frame = jnp.arange(rows, dtype=jnp.int32) // POOL
    own_seg = lax.dynamic_slice_in_dim(seg_rows, start, out_rows)
    own_frame = lax.dynamic_slice_in_dim(row_frame, start, out_rows)
    allowed = (seg_rows[None, :] == own_seg[:, None]) & (row_frame[None, :] <= own_frame[:, None])
    logits = jnp.einsum("rhd,khd->hrk", tquery, tkey, preferred_element_type=jnp.float32) * scale
    weights = jnp.where(allowed[None], jnp.exp(logits), jnp.float32(0.0))
    numer = jnp.einsum(
        "hrk,khd->rhd", weights.astype(jnp.bfloat16), tvalue, preferred_element_type=jnp.float32
    )
    denom = jnp.sum(weights, axis=-1)
    summary = numer / jnp.transpose(denom)[:, :, None]
    return summary.reshape(out_rows, t_heads * HD).astype(jnp.bfloat16)


def solution(mesh):
    return jax.shard_map(
        per_device,
        mesh=mesh,
        in_specs=(
            P(("groups", "video"), None, None),
            P(("groups", "video")),
            P("video", None, "tensor"),
            P("tensor", None, "video"),
        ),
        out_specs=P(("groups", "video"), "tensor"),
        check_vma=False,
    )
```

```python
import math

import jax
import jax.numpy as jnp
from jax import lax
from jax.sharding import PartitionSpec as P

HD = 128
PATCH = 256
POOL = 16


def rms_norm(values):
    return values * lax.rsqrt(jnp.mean(values * values, axis=-1, keepdims=True) + 1e-06)


def head_chunks(heads):
    if heads >= 4 and heads % 2 == 0:
        return [1] + [2] * ((heads - 2) // 2) + [1]
    return [1] * heads


def moved_weights(chunk, n_video, after=None):
    v = lax.axis_index("video")
    g = lax.axis_index("groups")
    half = chunk.shape[0] // 2
    mine = lax.dynamic_slice_in_dim(chunk, g * half, half, axis=0)
    if after is not None:
        mine, after = lax.optimization_barrier((mine, after))
    other = lax.dynamic_slice_in_dim(chunk, (1 - g) * half, half, axis=0)
    gathered = lax.all_gather(mine, "video", axis=0, tiled=True)
    onward = jnp.concatenate(
        [lax.dynamic_slice_in_dim(gathered, ((v + 1 + i) % n_video) * half, half, axis=0)
         for i in range(n_video - 1)], axis=0
    )
    return [other, gathered, onward], after


def forward(onward):
    return lax.ppermute(onward, "groups", [(0, 1), (1, 0)])


def attend(proj, nframes, heads, scale, blocks, inner):
    proj = proj.reshape(nframes, PATCH, 3, heads, HD)
    query = rms_norm(proj[:, :, 0]).astype(jnp.bfloat16)
    keys = rms_norm(proj[:, :, 1]).astype(jnp.bfloat16)
    values = proj[:, :, 2].astype(jnp.bfloat16)
    scores = jnp.einsum("fphd,fkhd->fhpk", query, keys, preferred_element_type=jnp.float32) * scale
    probs = jnp.exp(scores)
    probs = (probs / jnp.sum(probs, axis=-1, keepdims=True)).astype(jnp.bfloat16)
    attended = jnp.einsum("fhpk,fkhd->fphd", probs, values, preferred_element_type=jnp.float32)
    grid = attended.reshape(nframes, blocks, inner, blocks, inner, heads, HD)
    return jnp.mean(grid, axis=(2, 4)).reshape(nframes * POOL, heads * HD).astype(jnp.bfloat16)


def per_device(frames, frame_video, qkv_weight, conn_weight):
    scale = 1.0 / math.sqrt(HD)
    blocks = math.isqrt(POOL)
    inner = math.isqrt(PATCH) // blocks
    nframes = frames.shape[0]
    patch_rows = nframes * PATCH
    n_video = lax.axis_size("video")
    assert lax.axis_size("groups") == 2
    v = lax.axis_index("video")
    g = lax.axis_index("groups")
    heads_local = qkv_weight.shape[2] // HD
    sizes = head_chunks(heads_local)
    moved = []
    first = 0
    for size in sizes:
        chunk = qkv_weight[:, :, first * HD:(first + size) * HD]
        first += size
        if len(moved) == len(sizes) - 1 and len(sizes) > 2:
            whole_rows, moved[-1][1] = lax.optimization_barrier((chunk, moved[-1][1]))
            step = [lax.all_gather(whole_rows, "video", axis=0, tiled=True), None, None]
        elif moved:
            step, moved[-1][1] = moved_weights(chunk, n_video, after=moved[-1][1])
            step.append(forward(step[2]))
        else:
            step, _ = moved_weights(chunk, n_video)
            step.append(forward(step[2]))
            step[3], frames = lax.optimization_barrier((step[3], frames))
        moved.append(step)
    wide = frames.astype(jnp.float32)
    center = wide - jnp.mean(wide, axis=-1, keepdims=True)
    normed = center * lax.rsqrt(jnp.mean(center * center, axis=-1, keepdims=True) + 1e-06)
    normed = normed.astype(jnp.bfloat16).reshape(patch_rows, frames.shape[2])
    local_rows = qkv_weight.shape[0]
    half = local_rows // 2

    def columns(shard, which):
        return lax.dynamic_slice_in_dim(normed, shard * local_rows + which * half, half, axis=1)

    own_half = jnp.concatenate([columns(u, g) for u in range(n_video)], axis=1)
    own_piece = columns(v, 1 - g)
    rolled = jnp.concatenate(
        [columns((v + 1 + i) % n_video, 1 - g) for i in range(n_video - 1)], axis=1
    )
    if len(moved) > 2 and moved[1][3] is not None:
        moved[1][3], own_half = lax.optimization_barrier((moved[1][3], own_half))
        moved[2][1], own_half = lax.optimization_barrier((moved[2][1], own_half))
    video_all = lax.all_gather(frame_video, "video", axis=0, tiled=True)
    pooled_parts = []
    for index, size in enumerate(sizes):
        width = 3 * size * HD
        if moved[index][1] is None:
            full = moved[index][0].reshape(n_video * 2 * half, width)
            proj = jnp.dot(normed, full, preferred_element_type=jnp.float32)
            pooled_parts.append(attend(proj, nframes, size, scale, blocks, inner))
            continue
        other, gathered, onward, received = moved[index]
        if index == 0:
            video_all, received = lax.optimization_barrier((video_all, received))
        proj = jnp.dot(own_piece, other.reshape(half, width), preferred_element_type=jnp.float32)
        proj = proj + jnp.dot(
            own_half, gathered.reshape(n_video * half, width), preferred_element_type=jnp.float32
        )
        proj = proj + jnp.dot(
            rolled, received.reshape((n_video - 1) * half, width),
            preferred_element_type=jnp.float32,
        )
        pooled_parts.append(attend(proj, nframes, size, scale, blocks, inner))
    pooled = jnp.concatenate(pooled_parts, axis=1)
    pooled_all = lax.all_gather(pooled, "video", axis=0, tiled=True)
    rows = pooled_all.shape[0]
    partial_proj = jnp.einsum(
        "rc,ckt->rkt", pooled_all, conn_weight, preferred_element_type=jnp.float32
    )
    clip_rows = lax.psum_scatter(
        partial_proj.astype(jnp.bfloat16), "tensor", scatter_dimension=0, tiled=True
    )
    n_tensor = lax.axis_size("tensor")
    if n_video == n_tensor:
        t = lax.axis_index("tensor")
        pieces = [None] * n_tensor
        for k in range(n_tensor):
            pairs = [(a * n_tensor + b, ((b + k) % n_tensor) * n_tensor + a)
                     for a in range(n_video) for b in range(n_tensor)]
            got = lax.ppermute(clip_rows, ("video", "tensor"), pairs)
            pieces[k] = got
        source = [(v - k) % n_tensor for k in range(n_tensor)]
        stacked = jnp.stack(pieces, axis=0)
        order = jnp.argsort(jnp.stack(source))
        clip_proj = jnp.take(stacked, order, axis=0).reshape(rows, 3, -1).astype(jnp.float32)
    else:
        clip_rows = lax.all_gather(clip_rows, "video", axis=0, tiled=False)
        sub = n_video // n_tensor
        clip_rows = clip_rows.reshape((n_tensor, sub) + clip_rows.shape[1:])
        clip_proj = lax.all_to_all(clip_rows, "tensor", 0, 0, tiled=False)
        clip_proj = jnp.transpose(clip_proj, (0, 2, 3, 1, 4))
        clip_proj = clip_proj.reshape(rows, 3, -1).astype(jnp.float32)
    t_heads = clip_proj.shape[2] // HD
    out_rows = rows // n_video
    start = v * out_rows
    own = lax.dynamic_slice_in_dim(clip_proj[:, 0], start, out_rows, axis=0)
    tquery = rms_norm(own.reshape(out_rows, t_heads, HD)).astype(jnp.bfloat16)
    tkey = rms_norm(clip_proj[:, 1].reshape(rows, t_heads, HD)).astype(jnp.bfloat16)
    tvalue = clip_proj[:, 2].reshape(rows, t_heads, HD).astype(jnp.bfloat16)
    seg_rows = jnp.repeat(video_all, POOL)
    row_frame = jnp.arange(rows, dtype=jnp.int32) // POOL
    own_seg = lax.dynamic_slice_in_dim(seg_rows, start, out_rows)
    own_frame = lax.dynamic_slice_in_dim(row_frame, start, out_rows)
    allowed = (seg_rows[None, :] == own_seg[:, None]) & (row_frame[None, :] <= own_frame[:, None])
    logits = jnp.einsum("rhd,khd->hrk", tquery, tkey, preferred_element_type=jnp.float32) * scale
    weights = jnp.where(allowed[None], jnp.exp(logits), jnp.float32(0.0))
    numer = jnp.einsum(
        "hrk,khd->rhd", weights.astype(jnp.bfloat16), tvalue, preferred_element_type=jnp.float32
    )
    denom = jnp.sum(weights, axis=-1)
    summary = numer / jnp.transpose(denom)[:, :, None]
    return summary.reshape(out_rows, t_heads * HD).astype(jnp.bfloat16)


def solution(mesh):
    return jax.shard_map(
        per_device,
        mesh=mesh,
        in_specs=(
            P(("groups", "video"), None, None),
            P(("groups", "video")),
            P("video", None, "tensor"),
            P("tensor", None, "video"),
        ),
        out_specs=P(("groups", "video"), "tensor"),
        check_vma=False,
    )
```

```python
import math

import jax
import jax.numpy as jnp
from jax import lax
from jax.sharding import PartitionSpec as P

HD = 128
PATCH = 256
POOL = 16


def rms_norm(values):
    return values * lax.rsqrt(jnp.mean(values * values, axis=-1, keepdims=True) + 1e-06)


def head_chunks(heads):
    if heads >= 4 and heads % 2 == 0:
        return [1] + [2] * ((heads - 2) // 2) + [1]
    return [1] * heads


def moved_weights(chunk, n_video, after=None):
    v = lax.axis_index("video")
    g = lax.axis_index("groups")
    half = chunk.shape[0] // 2
    mine = lax.dynamic_slice_in_dim(chunk, g * half, half, axis=0)
    if after is not None:
        mine, after = lax.optimization_barrier((mine, after))
    other = lax.dynamic_slice_in_dim(chunk, (1 - g) * half, half, axis=0)
    gathered = lax.all_gather(mine, "video", axis=0, tiled=True)
    onward = jnp.concatenate(
        [lax.dynamic_slice_in_dim(gathered, ((v + 1 + i) % n_video) * half, half, axis=0)
         for i in range(n_video - 1)], axis=0
    )
    return [other, gathered, onward], after


def forward(onward):
    return lax.ppermute(onward, "groups", [(0, 1), (1, 0)])


def attend(proj, nframes, heads, scale, blocks, inner):
    proj = proj.reshape(nframes, PATCH, 3, heads, HD)
    query = rms_norm(proj[:, :, 0]).astype(jnp.bfloat16)
    keys = rms_norm(proj[:, :, 1]).astype(jnp.bfloat16)
    values = proj[:, :, 2].astype(jnp.bfloat16)
    scores = jnp.einsum("fphd,fkhd->fhpk", query, keys, preferred_element_type=jnp.float32) * scale
    probs = jnp.exp(scores)
    probs = (probs / jnp.sum(probs, axis=-1, keepdims=True)).astype(jnp.bfloat16)
    attended = jnp.einsum("fhpk,fkhd->fphd", probs, values, preferred_element_type=jnp.float32)
    grid = attended.reshape(nframes, blocks, inner, blocks, inner, heads, HD)
    return jnp.mean(grid, axis=(2, 4)).reshape(nframes * POOL, heads * HD).astype(jnp.bfloat16)


def per_device(frames, frame_video, qkv_weight, conn_weight):
    scale = 1.0 / math.sqrt(HD)
    blocks = math.isqrt(POOL)
    inner = math.isqrt(PATCH) // blocks
    nframes = frames.shape[0]
    patch_rows = nframes * PATCH
    n_video = lax.axis_size("video")
    assert lax.axis_size("groups") == 2
    v = lax.axis_index("video")
    g = lax.axis_index("groups")
    heads_local = qkv_weight.shape[2] // HD
    sizes = head_chunks(heads_local)
    moved = []
    first = 0
    for size in sizes:
        chunk = qkv_weight[:, :, first * HD:(first + size) * HD]
        first += size
        if len(moved) == len(sizes) - 1 and len(sizes) > 2:
            whole_rows, moved[-2][1] = lax.optimization_barrier((chunk, moved[-2][1]))
            step = [lax.all_gather(whole_rows, "video", axis=0, tiled=True), None, None]
        elif moved:
            step, moved[-1][1] = moved_weights(chunk, n_video, after=moved[-1][1])
            step.append(forward(step[2]))
        else:
            step, _ = moved_weights(chunk, n_video)
            step.append(forward(step[2]))
            step[3], frames = lax.optimization_barrier((step[3], frames))
        moved.append(step)
    wide = frames.astype(jnp.float32)
    center = wide - jnp.mean(wide, axis=-1, keepdims=True)
    normed = center * lax.rsqrt(jnp.mean(center * center, axis=-1, keepdims=True) + 1e-06)
    normed = normed.astype(jnp.bfloat16).reshape(patch_rows, frames.shape[2])
    local_rows = qkv_weight.shape[0]
    half = local_rows // 2

    def columns(shard, which):
        return lax.dynamic_slice_in_dim(normed, shard * local_rows + which * half, half, axis=1)

    own_half = jnp.concatenate([columns(u, g) for u in range(n_video)], axis=1)
    own_piece = columns(v, 1 - g)
    rolled = jnp.concatenate(
        [columns((v + 1 + i) % n_video, 1 - g) for i in range(n_video - 1)], axis=1
    )
    if len(moved) > 2 and moved[1][3] is not None:
        moved[1][3], own_half = lax.optimization_barrier((moved[1][3], own_half))
    video_all = lax.all_gather(frame_video, "video", axis=0, tiled=True)
    pooled_parts = []
    for index, size in enumerate(sizes):
        width = 3 * size * HD
        if moved[index][1] is None:
            full = moved[index][0].reshape(n_video * 2 * half, width)
            proj = jnp.dot(normed, full, preferred_element_type=jnp.float32)
            pooled_parts.append(attend(proj, nframes, size, scale, blocks, inner))
            continue
        other, gathered, onward, received = moved[index]
        if index == 0:
            video_all, received = lax.optimization_barrier((video_all, received))
        proj = jnp.dot(own_piece, other.reshape(half, width), preferred_element_type=jnp.float32)
        proj = proj + jnp.dot(
            own_half, gathered.reshape(n_video * half, width), preferred_element_type=jnp.float32
        )
        proj = proj + jnp.dot(
            rolled, received.reshape((n_video - 1) * half, width),
            preferred_element_type=jnp.float32,
        )
        pooled_parts.append(attend(proj, nframes, size, scale, blocks, inner))
    pooled = jnp.concatenate(pooled_parts, axis=1)
    pooled_all = lax.all_gather(pooled, "video", axis=0, tiled=True)
    rows = pooled_all.shape[0]
    partial_proj = jnp.einsum(
        "rc,ckt->rkt", pooled_all, conn_weight, preferred_element_type=jnp.float32
    )
    clip_rows = lax.psum_scatter(
        partial_proj.astype(jnp.bfloat16), "tensor", scatter_dimension=0, tiled=True
    )
    n_tensor = lax.axis_size("tensor")
    if n_video == n_tensor:
        t = lax.axis_index("tensor")
        pieces = [None] * n_tensor
        for k in range(n_tensor):
            pairs = [(a * n_tensor + b, ((b + k) % n_tensor) * n_tensor + a)
                     for a in range(n_video) for b in range(n_tensor)]
            got = lax.ppermute(clip_rows, ("video", "tensor"), pairs)
            pieces[k] = got
        source = [(v - k) % n_tensor for k in range(n_tensor)]
        stacked = jnp.stack(pieces, axis=0)
        order = jnp.argsort(jnp.stack(source))
        clip_proj = jnp.take(stacked, order, axis=0).reshape(rows, 3, -1).astype(jnp.float32)
    else:
        clip_rows = lax.all_gather(clip_rows, "video", axis=0, tiled=False)
        sub = n_video // n_tensor
        clip_rows = clip_rows.reshape((n_tensor, sub) + clip_rows.shape[1:])
        clip_proj = lax.all_to_all(clip_rows, "tensor", 0, 0, tiled=False)
        clip_proj = jnp.transpose(clip_proj, (0, 2, 3, 1, 4))
        clip_proj = clip_proj.reshape(rows, 3, -1).astype(jnp.float32)
    t_heads = clip_proj.shape[2] // HD
    out_rows = rows // n_video
    start = v * out_rows
    own = lax.dynamic_slice_in_dim(clip_proj[:, 0], start, out_rows, axis=0)
    tquery = rms_norm(own.reshape(out_rows, t_heads, HD)).astype(jnp.bfloat16)
    tkey = rms_norm(clip_proj[:, 1].reshape(rows, t_heads, HD)).astype(jnp.bfloat16)
    tvalue = clip_proj[:, 2].reshape(rows, t_heads, HD).astype(jnp.bfloat16)
    seg_rows = jnp.repeat(video_all, POOL)
    row_frame = jnp.arange(rows, dtype=jnp.int32) // POOL
    own_seg = lax.dynamic_slice_in_dim(seg_rows, start, out_rows)
    own_frame = lax.dynamic_slice_in_dim(row_frame, start, out_rows)
    allowed = (seg_rows[None, :] == own_seg[:, None]) & (row_frame[None, :] <= own_frame[:, None])
    logits = jnp.einsum("rhd,khd->hrk", tquery, tkey, preferred_element_type=jnp.float32) * scale
    weights = jnp.where(allowed[None], jnp.exp(logits), jnp.float32(0.0))
    numer = jnp.einsum(
        "hrk,khd->rhd", weights.astype(jnp.bfloat16), tvalue, preferred_element_type=jnp.float32
    )
    denom = jnp.sum(weights, axis=-1)
    summary = numer / jnp.transpose(denom)[:, :, None]
    return summary.reshape(out_rows, t_heads * HD).astype(jnp.bfloat16)


def solution(mesh):
    return jax.shard_map(
        per_device,
        mesh=mesh,
        in_specs=(
            P(("groups", "video"), None, None),
            P(("groups", "video")),
            P("video", None, "tensor"),
            P("tensor", None, "video"),
        ),
        out_specs=P(("groups", "video"), "tensor"),
        check_vma=False,
    )
```

```python
import math

import jax
import jax.numpy as jnp
from jax import lax
from jax.sharding import PartitionSpec as P

HD = 128
PATCH = 256
POOL = 16


def rms_norm(values):
    return values * lax.rsqrt(jnp.mean(values * values, axis=-1, keepdims=True) + 1e-06)


def head_chunks(heads):
    if heads >= 4 and heads % 2 == 0:
        return [1] + [2] * ((heads - 2) // 2) + [1]
    return [1] * heads


def moved_weights(chunk, n_video, after=None):
    v = lax.axis_index("video")
    g = lax.axis_index("groups")
    half = chunk.shape[0] // 2
    mine = lax.dynamic_slice_in_dim(chunk, g * half, half, axis=0)
    if after is not None:
        mine, after = lax.optimization_barrier((mine, after))
    other = lax.dynamic_slice_in_dim(chunk, (1 - g) * half, half, axis=0)
    gathered = lax.all_gather(mine, "video", axis=0, tiled=True)
    onward = jnp.concatenate(
        [lax.dynamic_slice_in_dim(gathered, ((v + 1 + i) % n_video) * half, half, axis=0)
         for i in range(n_video - 1)], axis=0
    )
    return [other, gathered, onward], after


def forward(onward):
    return lax.ppermute(onward, "groups", [(0, 1), (1, 0)])


def attend(proj, nframes, heads, scale, blocks, inner):
    proj = proj.reshape(nframes, PATCH, 3, heads, HD)
    query = rms_norm(proj[:, :, 0]).astype(jnp.bfloat16)
    keys = rms_norm(proj[:, :, 1]).astype(jnp.bfloat16)
    values = proj[:, :, 2].astype(jnp.bfloat16)
    scores = jnp.einsum("fphd,fkhd->fhpk", query, keys, preferred_element_type=jnp.float32) * scale
    probs = jnp.exp(scores)
    probs = (probs / jnp.sum(probs, axis=-1, keepdims=True)).astype(jnp.bfloat16)
    attended = jnp.einsum("fhpk,fkhd->fphd", probs, values, preferred_element_type=jnp.float32)
    grid = attended.reshape(nframes, blocks, inner, blocks, inner, heads, HD)
    return jnp.mean(grid, axis=(2, 4)).reshape(nframes * POOL, heads * HD).astype(jnp.bfloat16)


def per_device(frames, frame_video, qkv_weight, conn_weight):
    scale = 1.0 / math.sqrt(HD)
    blocks = math.isqrt(POOL)
    inner = math.isqrt(PATCH) // blocks
    nframes = frames.shape[0]
    patch_rows = nframes * PATCH
    n_video = lax.axis_size("video")
    assert lax.axis_size("groups") == 2
    v = lax.axis_index("video")
    g = lax.axis_index("groups")
    heads_local = qkv_weight.shape[2] // HD
    sizes = head_chunks(heads_local)
    moved = []
    first = 0
    for size in sizes:
        chunk = qkv_weight[:, :, first * HD:(first + size) * HD]
        first += size
        if len(moved) == len(sizes) - 1 and len(sizes) > 2:
            whole_rows, moved[-1][1] = lax.optimization_barrier((chunk, moved[-1][1]))
            step = [lax.all_gather(whole_rows, "video", axis=0, tiled=True), None, None]
        elif moved:
            step, moved[-1][1] = moved_weights(chunk, n_video, after=moved[-1][1])
            step.append(forward(step[2]))
        else:
            step, _ = moved_weights(chunk, n_video)
            step.append(forward(step[2]))
            step[3], frames = lax.optimization_barrier((step[3], frames))
        moved.append(step)
    wide = frames.astype(jnp.float32)
    center = wide - jnp.mean(wide, axis=-1, keepdims=True)
    normed = center * lax.rsqrt(jnp.mean(center * center, axis=-1, keepdims=True) + 1e-06)
    normed = normed.astype(jnp.bfloat16).reshape(patch_rows, frames.shape[2])
    local_rows = qkv_weight.shape[0]
    half = local_rows // 2

    def columns(shard, which):
        return lax.dynamic_slice_in_dim(normed, shard * local_rows + which * half, half, axis=1)

    own_half = jnp.concatenate([columns(u, g) for u in range(n_video)], axis=1)
    own_piece = columns(v, 1 - g)
    rolled = jnp.concatenate(
        [columns((v + 1 + i) % n_video, 1 - g) for i in range(n_video - 1)], axis=1
    )
    if len(moved) > 2 and moved[1][3] is not None:
        moved[1][3], own_half = lax.optimization_barrier((moved[1][3], own_half))
    video_all = lax.all_gather(frame_video, "video", axis=0, tiled=True)
    pooled_parts = []
    for index, size in enumerate(sizes):
        width = 3 * size * HD
        if moved[index][1] is None:
            full = moved[index][0].reshape(n_video * 2 * half, width)
            proj = jnp.dot(normed, full, preferred_element_type=jnp.float32)
            pooled_parts.append(attend(proj, nframes, size, scale, blocks, inner))
            continue
        other, gathered, onward, received = moved[index]
        if index == 0:
            video_all, received = lax.optimization_barrier((video_all, received))
        proj = jnp.dot(own_piece, other.reshape(half, width), preferred_element_type=jnp.float32)
        proj = proj + jnp.dot(
            own_half, gathered.reshape(n_video * half, width), preferred_element_type=jnp.float32
        )
        proj = proj + jnp.dot(
            rolled, received.reshape((n_video - 1) * half, width),
            preferred_element_type=jnp.float32,
        )
        pooled_parts.append(attend(proj, nframes, size, scale, blocks, inner))
    pooled = jnp.concatenate(pooled_parts, axis=1)
    shifted = [pooled] + [
        lax.ppermute(pooled, "video", [(a, (a + k) % n_video) for a in range(n_video)])
        for k in range(1, n_video)
    ]
    came_from = jnp.argsort(jnp.stack([(v - k) % n_video for k in range(n_video)]))
    pooled_all = jnp.take(jnp.stack(shifted), came_from, axis=0).reshape(-1, pooled.shape[1])
    rows = pooled_all.shape[0]
    partial_proj = jnp.einsum(
        "rc,ckt->rkt", pooled_all, conn_weight, preferred_element_type=jnp.float32
    )
    clip_rows = lax.psum_scatter(
        partial_proj.astype(jnp.bfloat16), "tensor", scatter_dimension=0, tiled=True
    )
    n_tensor = lax.axis_size("tensor")
    if n_video == n_tensor:
        t = lax.axis_index("tensor")
        pieces = [None] * n_tensor
        for k in range(n_tensor):
            pairs = [(a * n_tensor + b, ((b + k) % n_tensor) * n_tensor + a)
                     for a in range(n_video) for b in range(n_tensor)]
            got = lax.ppermute(clip_rows, ("video", "tensor"), pairs)
            pieces[k] = got
        source = [(v - k) % n_tensor for k in range(n_tensor)]
        stacked = jnp.stack(pieces, axis=0)
        order = jnp.argsort(jnp.stack(source))
        clip_proj = jnp.take(stacked, order, axis=0).reshape(rows, 3, -1).astype(jnp.float32)
    else:
        clip_rows = lax.all_gather(clip_rows, "video", axis=0, tiled=False)
        sub = n_video // n_tensor
        clip_rows = clip_rows.reshape((n_tensor, sub) + clip_rows.shape[1:])
        clip_proj = lax.all_to_all(clip_rows, "tensor", 0, 0, tiled=False)
        clip_proj = jnp.transpose(clip_proj, (0, 2, 3, 1, 4))
        clip_proj = clip_proj.reshape(rows, 3, -1).astype(jnp.float32)
    t_heads = clip_proj.shape[2] // HD
    out_rows = rows // n_video
    start = v * out_rows
    own = lax.dynamic_slice_in_dim(clip_proj[:, 0], start, out_rows, axis=0)
    tquery = rms_norm(own.reshape(out_rows, t_heads, HD)).astype(jnp.bfloat16)
    tkey = rms_norm(clip_proj[:, 1].reshape(rows, t_heads, HD)).astype(jnp.bfloat16)
    tvalue = clip_proj[:, 2].reshape(rows, t_heads, HD).astype(jnp.bfloat16)
    seg_rows = jnp.repeat(video_all, POOL)
    row_frame = jnp.arange(rows, dtype=jnp.int32) // POOL
    own_seg = lax.dynamic_slice_in_dim(seg_rows, start, out_rows)
    own_frame = lax.dynamic_slice_in_dim(row_frame, start, out_rows)
    allowed = (seg_rows[None, :] == own_seg[:, None]) & (row_frame[None, :] <= own_frame[:, None])
    logits = jnp.einsum("rhd,khd->hrk", tquery, tkey, preferred_element_type=jnp.float32) * scale
    weights = jnp.where(allowed[None], jnp.exp(logits), jnp.float32(0.0))
    numer = jnp.einsum(
        "hrk,khd->rhd", weights.astype(jnp.bfloat16), tvalue, preferred_element_type=jnp.float32
    )
    denom = jnp.sum(weights, axis=-1)
    summary = numer / jnp.transpose(denom)[:, :, None]
    return summary.reshape(out_rows, t_heads * HD).astype(jnp.bfloat16)


def solution(mesh):
    return jax.shard_map(
        per_device,
        mesh=mesh,
        in_specs=(
            P(("groups", "video"), None, None),
            P(("groups", "video")),
            P("video", None, "tensor"),
            P("tensor", None, "video"),
        ),
        out_specs=P(("groups", "video"), "tensor"),
        check_vma=False,
    )
```

```python
import math

import jax
import jax.numpy as jnp
from jax import lax
from jax.sharding import PartitionSpec as P

HD = 128
PATCH = 256
POOL = 16


def rms_norm(values):
    return values * lax.rsqrt(jnp.mean(values * values, axis=-1, keepdims=True) + 1e-06)


def head_chunks(heads):
    if heads >= 4 and heads % 2 == 0:
        return [1] + [2] * ((heads - 2) // 2) + [1]
    return [1] * heads


def moved_weights(chunk, n_video, after=None):
    v = lax.axis_index("video")
    g = lax.axis_index("groups")
    half = chunk.shape[0] // 2
    mine = lax.dynamic_slice_in_dim(chunk, g * half, half, axis=0)
    if after is not None:
        mine, after = lax.optimization_barrier((mine, after))
    other = lax.dynamic_slice_in_dim(chunk, (1 - g) * half, half, axis=0)
    gathered = lax.all_gather(mine, "video", axis=0, tiled=True)
    onward = jnp.concatenate(
        [lax.dynamic_slice_in_dim(gathered, ((v + 1 + i) % n_video) * half, half, axis=0)
         for i in range(n_video - 1)], axis=0
    )
    return [other, gathered, onward], after


def forward(onward):
    return lax.ppermute(onward, "groups", [(0, 1), (1, 0)])


def attend(proj, nframes, heads, scale, blocks, inner):
    proj = proj.reshape(nframes, PATCH, 3, heads, HD)
    query = rms_norm(proj[:, :, 0]).astype(jnp.bfloat16)
    keys = rms_norm(proj[:, :, 1]).astype(jnp.bfloat16)
    values = proj[:, :, 2].astype(jnp.bfloat16)
    scores = jnp.einsum("fphd,fkhd->fhpk", query, keys, preferred_element_type=jnp.float32) * scale
    probs = jnp.exp(scores)
    probs = (probs / jnp.sum(probs, axis=-1, keepdims=True)).astype(jnp.bfloat16)
    attended = jnp.einsum("fhpk,fkhd->fphd", probs, values, preferred_element_type=jnp.float32)
    grid = attended.reshape(nframes, blocks, inner, blocks, inner, heads, HD)
    return jnp.mean(grid, axis=(2, 4)).reshape(nframes * POOL, heads * HD).astype(jnp.bfloat16)


def per_device(frames, frame_video, qkv_weight, conn_weight):
    scale = 1.0 / math.sqrt(HD)
    blocks = math.isqrt(POOL)
    inner = math.isqrt(PATCH) // blocks
    nframes = frames.shape[0]
    patch_rows = nframes * PATCH
    n_video = lax.axis_size("video")
    assert lax.axis_size("groups") == 2
    v = lax.axis_index("video")
    g = lax.axis_index("groups")
    heads_local = qkv_weight.shape[2] // HD
    sizes = head_chunks(heads_local)
    moved = []
    first = 0
    for size in sizes:
        chunk = qkv_weight[:, :, first * HD:(first + size) * HD]
        first += size
        if len(moved) == len(sizes) - 1 and len(sizes) > 2:
            whole_rows, moved[-1][1] = lax.optimization_barrier((chunk, moved[-1][1]))
            step = [lax.all_gather(whole_rows, "video", axis=0, tiled=True), None, None]
        elif moved:
            step, moved[-1][1] = moved_weights(chunk, n_video, after=moved[-1][1])
            step.append(forward(step[2]))
        else:
            step, _ = moved_weights(chunk, n_video)
            step.append(forward(step[2]))
            step[3], frames = lax.optimization_barrier((step[3], frames))
        moved.append(step)
    wide = frames.astype(jnp.float32)
    center = wide - jnp.mean(wide, axis=-1, keepdims=True)
    normed = center * lax.rsqrt(jnp.mean(center * center, axis=-1, keepdims=True) + 1e-06)
    normed = normed.astype(jnp.bfloat16).reshape(patch_rows, frames.shape[2])
    local_rows = qkv_weight.shape[0]
    half = local_rows // 2

    def columns(shard, which):
        return lax.dynamic_slice_in_dim(normed, shard * local_rows + which * half, half, axis=1)

    own_half = jnp.concatenate([columns(u, g) for u in range(n_video)], axis=1)
    own_piece = columns(v, 1 - g)
    rolled = jnp.concatenate(
        [columns((v + 1 + i) % n_video, 1 - g) for i in range(n_video - 1)], axis=1
    )
    if len(moved) > 2 and moved[1][3] is not None:
        moved[1][3], own_half = lax.optimization_barrier((moved[1][3], own_half))
    video_all = lax.all_gather(frame_video, "video", axis=0, tiled=True)
    pooled_parts = []
    for index, size in enumerate(sizes):
        width = 3 * size * HD
        if moved[index][1] is None:
            full = moved[index][0].reshape(n_video * 2 * half, width)
            proj = jnp.dot(normed, full, preferred_element_type=jnp.float32)
            pooled_parts.append(attend(proj, nframes, size, scale, blocks, inner))
            continue
        other, gathered, onward, received = moved[index]
        if index == 0:
            video_all, received = lax.optimization_barrier((video_all, received))
        proj = jnp.dot(own_piece, other.reshape(half, width), preferred_element_type=jnp.float32)
        proj = proj + jnp.dot(
            own_half, gathered.reshape(n_video * half, width), preferred_element_type=jnp.float32
        )
        proj = proj + jnp.dot(
            rolled, received.reshape((n_video - 1) * half, width),
            preferred_element_type=jnp.float32,
        )
        pooled_parts.append(attend(proj, nframes, size, scale, blocks, inner))
    pooled = jnp.concatenate(pooled_parts, axis=1)
    shifted = [pooled] + [
        lax.ppermute(pooled, "video", [(a, (a + k) % n_video) for a in range(n_video)])
        for k in range(1, n_video)
    ]
    came_from = jnp.argsort(jnp.stack([(v - k) % n_video for k in range(n_video)]))
    pooled_all = jnp.take(jnp.stack(shifted), came_from, axis=0).reshape(-1, pooled.shape[1])
    rows = pooled_all.shape[0]
    partial_proj = jnp.einsum(
        "rc,ckt->rkt", pooled_all, conn_weight, preferred_element_type=jnp.float32
    )
    n_tensor = lax.axis_size("tensor")
    t = lax.axis_index("tensor")
    sent = partial_proj.astype(jnp.bfloat16)
    block = rows // n_tensor
    total = lax.dynamic_slice_in_dim(sent, t * block, block, axis=0).astype(jnp.float32)
    for k in range(1, n_tensor):
        piece = lax.dynamic_slice_in_dim(sent, ((t + k) % n_tensor) * block, block, axis=0)
        got = lax.ppermute(piece, "tensor", [(a, (a + k) % n_tensor) for a in range(n_tensor)])
        total = total + got.astype(jnp.float32)
    clip_rows = total.astype(jnp.bfloat16)
    if n_video == n_tensor:
        pieces = [None] * n_tensor
        for k in range(n_tensor):
            pairs = [(a * n_tensor + b, ((b + k) % n_tensor) * n_tensor + a)
                     for a in range(n_video) for b in range(n_tensor)]
            got = lax.ppermute(clip_rows, ("video", "tensor"), pairs)
            pieces[k] = got
        source = [(v - k) % n_tensor for k in range(n_tensor)]
        stacked = jnp.stack(pieces, axis=0)
        order = jnp.argsort(jnp.stack(source))
        clip_proj = jnp.take(stacked, order, axis=0).reshape(rows, 3, -1).astype(jnp.float32)
    else:
        clip_rows = lax.all_gather(clip_rows, "video", axis=0, tiled=False)
        sub = n_video // n_tensor
        clip_rows = clip_rows.reshape((n_tensor, sub) + clip_rows.shape[1:])
        clip_proj = lax.all_to_all(clip_rows, "tensor", 0, 0, tiled=False)
        clip_proj = jnp.transpose(clip_proj, (0, 2, 3, 1, 4))
        clip_proj = clip_proj.reshape(rows, 3, -1).astype(jnp.float32)
    t_heads = clip_proj.shape[2] // HD
    out_rows = rows // n_video
    start = v * out_rows
    own = lax.dynamic_slice_in_dim(clip_proj[:, 0], start, out_rows, axis=0)
    tquery = rms_norm(own.reshape(out_rows, t_heads, HD)).astype(jnp.bfloat16)
    tkey = rms_norm(clip_proj[:, 1].reshape(rows, t_heads, HD)).astype(jnp.bfloat16)
    tvalue = clip_proj[:, 2].reshape(rows, t_heads, HD).astype(jnp.bfloat16)
    seg_rows = jnp.repeat(video_all, POOL)
    row_frame = jnp.arange(rows, dtype=jnp.int32) // POOL
    own_seg = lax.dynamic_slice_in_dim(seg_rows, start, out_rows)
    own_frame = lax.dynamic_slice_in_dim(row_frame, start, out_rows)
    allowed = (seg_rows[None, :] == own_seg[:, None]) & (row_frame[None, :] <= own_frame[:, None])
    logits = jnp.einsum("rhd,khd->hrk", tquery, tkey, preferred_element_type=jnp.float32) * scale
    weights = jnp.where(allowed[None], jnp.exp(logits), jnp.float32(0.0))
    numer = jnp.einsum(
        "hrk,khd->rhd", weights.astype(jnp.bfloat16), tvalue, preferred_element_type=jnp.float32
    )
    denom = jnp.sum(weights, axis=-1)
    summary = numer / jnp.transpose(denom)[:, :, None]
    return summary.reshape(out_rows, t_heads * HD).astype(jnp.bfloat16)


def solution(mesh):
    return jax.shard_map(
        per_device,
        mesh=mesh,
        in_specs=(
            P(("groups", "video"), None, None),
            P(("groups", "video")),
            P("video", None, "tensor"),
            P("tensor", None, "video"),
        ),
        out_specs=P(("groups", "video"), "tensor"),
        check_vma=False,
    )
```

```python
import math

import jax
import jax.numpy as jnp
from jax import lax
from jax.sharding import PartitionSpec as P

HD = 128
PATCH = 256
POOL = 16


def rms_norm(values):
    return values * lax.rsqrt(jnp.mean(values * values, axis=-1, keepdims=True) + 1e-06)


def head_chunks(heads):
    if heads >= 4 and heads % 2 == 0:
        return [1] + [2] * ((heads - 2) // 2) + [1]
    return [1] * heads


def moved_weights(chunk, n_video, after=None):
    v = lax.axis_index("video")
    g = lax.axis_index("groups")
    half = chunk.shape[0] // 2
    mine = lax.dynamic_slice_in_dim(chunk, g * half, half, axis=0)
    if after is not None:
        mine, after = lax.optimization_barrier((mine, after))
    other = lax.dynamic_slice_in_dim(chunk, (1 - g) * half, half, axis=0)
    gathered = lax.all_gather(mine, "video", axis=0, tiled=True)
    onward = jnp.concatenate(
        [lax.dynamic_slice_in_dim(gathered, ((v + 1 + i) % n_video) * half, half, axis=0)
         for i in range(n_video - 1)], axis=0
    )
    return [other, gathered, onward], after


def forward(onward):
    return lax.ppermute(onward, "groups", [(0, 1), (1, 0)])


def attend(proj, nframes, heads, scale, blocks, inner):
    proj = proj.reshape(nframes, PATCH, 3, heads, HD)
    query = rms_norm(proj[:, :, 0]).astype(jnp.bfloat16)
    keys = rms_norm(proj[:, :, 1]).astype(jnp.bfloat16)
    values = proj[:, :, 2].astype(jnp.bfloat16)
    scores = jnp.einsum("fphd,fkhd->fhpk", query, keys, preferred_element_type=jnp.float32) * scale
    probs = jnp.exp(scores)
    probs = (probs / jnp.sum(probs, axis=-1, keepdims=True)).astype(jnp.bfloat16)
    attended = jnp.einsum("fhpk,fkhd->fphd", probs, values, preferred_element_type=jnp.float32)
    grid = attended.reshape(nframes, blocks, inner, blocks, inner, heads, HD)
    return jnp.mean(grid, axis=(2, 4)).reshape(nframes * POOL, heads * HD).astype(jnp.bfloat16)


def per_device(frames, frame_video, qkv_weight, conn_weight):
    scale = 1.0 / math.sqrt(HD)
    blocks = math.isqrt(POOL)
    inner = math.isqrt(PATCH) // blocks
    nframes = frames.shape[0]
    patch_rows = nframes * PATCH
    n_video = lax.axis_size("video")
    assert lax.axis_size("groups") == 2
    v = lax.axis_index("video")
    g = lax.axis_index("groups")
    heads_local = qkv_weight.shape[2] // HD
    sizes = head_chunks(heads_local)
    moved = []
    first = 0
    for size in sizes:
        chunk = qkv_weight[:, :, first * HD:(first + size) * HD]
        first += size
        if len(moved) == len(sizes) - 1 and len(sizes) > 2:
            whole_rows, moved[-1][1] = lax.optimization_barrier((chunk, moved[-1][1]))
            step = [lax.all_gather(whole_rows, "video", axis=0, tiled=True), None, None]
        elif moved:
            step, moved[-1][1] = moved_weights(chunk, n_video, after=moved[-1][1])
            step.append(forward(step[2]))
        else:
            step, _ = moved_weights(chunk, n_video)
            step.append(forward(step[2]))
            step[3], frames = lax.optimization_barrier((step[3], frames))
        moved.append(step)
    wide = frames.astype(jnp.float32)
    center = wide - jnp.mean(wide, axis=-1, keepdims=True)
    normed = center * lax.rsqrt(jnp.mean(center * center, axis=-1, keepdims=True) + 1e-06)
    normed = normed.astype(jnp.bfloat16).reshape(patch_rows, frames.shape[2])
    local_rows = qkv_weight.shape[0]
    half = local_rows // 2

    def columns(shard, which):
        return lax.dynamic_slice_in_dim(normed, shard * local_rows + which * half, half, axis=1)

    own_half = jnp.concatenate([columns(u, g) for u in range(n_video)], axis=1)
    own_piece = columns(v, 1 - g)
    rolled = jnp.concatenate(
        [columns((v + 1 + i) % n_video, 1 - g) for i in range(n_video - 1)], axis=1
    )
    if len(moved) > 2 and moved[1][3] is not None:
        moved[1][3], own_half = lax.optimization_barrier((moved[1][3], own_half))
    ids = [frame_video] + [
        lax.ppermute(frame_video, "video", [(a, (a + k) % n_video) for a in range(n_video)])
        for k in range(1, n_video)
    ]
    ids_from = jnp.argsort(jnp.stack([(v - k) % n_video for k in range(n_video)]))
    video_all = jnp.take(jnp.stack(ids), ids_from, axis=0).reshape(-1)
    pooled_parts = []
    for index, size in enumerate(sizes):
        width = 3 * size * HD
        if moved[index][1] is None:
            full = moved[index][0].reshape(n_video * 2 * half, width)
            proj = jnp.dot(normed, full, preferred_element_type=jnp.float32)
            pooled_parts.append(attend(proj, nframes, size, scale, blocks, inner))
            continue
        other, gathered, onward, received = moved[index]
        if index == 0:
            video_all, received = lax.optimization_barrier((video_all, received))
        proj = jnp.dot(own_piece, other.reshape(half, width), preferred_element_type=jnp.float32)
        proj = proj + jnp.dot(
            own_half, gathered.reshape(n_video * half, width), preferred_element_type=jnp.float32
        )
        proj = proj + jnp.dot(
            rolled, received.reshape((n_video - 1) * half, width),
            preferred_element_type=jnp.float32,
        )
        pooled_parts.append(attend(proj, nframes, size, scale, blocks, inner))
    pooled = jnp.concatenate(pooled_parts, axis=1)
    shifted = [pooled] + [
        lax.ppermute(pooled, "video", [(a, (a + k) % n_video) for a in range(n_video)])
        for k in range(1, n_video)
    ]
    came_from = jnp.argsort(jnp.stack([(v - k) % n_video for k in range(n_video)]))
    pooled_all = jnp.take(jnp.stack(shifted), came_from, axis=0).reshape(-1, pooled.shape[1])
    rows = pooled_all.shape[0]
    partial_proj = jnp.einsum(
        "rc,ckt->rkt", pooled_all, conn_weight, preferred_element_type=jnp.float32
    )
    n_tensor = lax.axis_size("tensor")
    t = lax.axis_index("tensor")
    sent = partial_proj.astype(jnp.bfloat16)
    block = rows // n_tensor
    total = lax.dynamic_slice_in_dim(sent, t * block, block, axis=0).astype(jnp.float32)
    for k in range(1, n_tensor):
        piece = lax.dynamic_slice_in_dim(sent, ((t + k) % n_tensor) * block, block, axis=0)
        got = lax.ppermute(piece, "tensor", [(a, (a + k) % n_tensor) for a in range(n_tensor)])
        total = total + got.astype(jnp.float32)
    clip_rows = total.astype(jnp.bfloat16)
    if n_video == n_tensor:
        pieces = [None] * n_tensor
        for k in range(n_tensor):
            pairs = [(a * n_tensor + b, ((b + k) % n_tensor) * n_tensor + a)
                     for a in range(n_video) for b in range(n_tensor)]
            got = lax.ppermute(clip_rows, ("video", "tensor"), pairs)
            pieces[k] = got
        source = [(v - k) % n_tensor for k in range(n_tensor)]
        stacked = jnp.stack(pieces, axis=0)
        order = jnp.argsort(jnp.stack(source))
        clip_proj = jnp.take(stacked, order, axis=0).reshape(rows, 3, -1).astype(jnp.float32)
    else:
        clip_rows = lax.all_gather(clip_rows, "video", axis=0, tiled=False)
        sub = n_video // n_tensor
        clip_rows = clip_rows.reshape((n_tensor, sub) + clip_rows.shape[1:])
        clip_proj = lax.all_to_all(clip_rows, "tensor", 0, 0, tiled=False)
        clip_proj = jnp.transpose(clip_proj, (0, 2, 3, 1, 4))
        clip_proj = clip_proj.reshape(rows, 3, -1).astype(jnp.float32)
    t_heads = clip_proj.shape[2] // HD
    out_rows = rows // n_video
    start = v * out_rows
    own = lax.dynamic_slice_in_dim(clip_proj[:, 0], start, out_rows, axis=0)
    tquery = rms_norm(own.reshape(out_rows, t_heads, HD)).astype(jnp.bfloat16)
    tkey = rms_norm(clip_proj[:, 1].reshape(rows, t_heads, HD)).astype(jnp.bfloat16)
    tvalue = clip_proj[:, 2].reshape(rows, t_heads, HD).astype(jnp.bfloat16)
    seg_rows = jnp.repeat(video_all, POOL)
    row_frame = jnp.arange(rows, dtype=jnp.int32) // POOL
    own_seg = lax.dynamic_slice_in_dim(seg_rows, start, out_rows)
    own_frame = lax.dynamic_slice_in_dim(row_frame, start, out_rows)
    allowed = (seg_rows[None, :] == own_seg[:, None]) & (row_frame[None, :] <= own_frame[:, None])
    logits = jnp.einsum("rhd,khd->hrk", tquery, tkey, preferred_element_type=jnp.float32) * scale
    weights = jnp.where(allowed[None], jnp.exp(logits), jnp.float32(0.0))
    numer = jnp.einsum(
        "hrk,khd->rhd", weights.astype(jnp.bfloat16), tvalue, preferred_element_type=jnp.float32
    )
    denom = jnp.sum(weights, axis=-1)
    summary = numer / jnp.transpose(denom)[:, :, None]
    return summary.reshape(out_rows, t_heads * HD).astype(jnp.bfloat16)


def solution(mesh):
    return jax.shard_map(
        per_device,
        mesh=mesh,
        in_specs=(
            P(("groups", "video"), None, None),
            P(("groups", "video")),
            P("video", None, "tensor"),
            P("tensor", None, "video"),
        ),
        out_specs=P(("groups", "video"), "tensor"),
        check_vma=False,
    )
```
